256 devices in a mesh: dp: 32 (over z, x), mp: 8 (over y, core).
Axes of the slice: x: 4, y: 4, z: 8, core: 2. Of those that a mesh axis runs over, the one named last changes fastest.
Arguments:
- token_ids: int32 [2048, 7], replicated, may hold values from 0 to 65535
- lengths: int32 [2048], replicated, may hold values from 1 to 7, as said below
- pack_dest: int32 [2048], replicated, may hold values from 0 to 31, as said below
- ref_hidden: bfloat16 [2048, 7, 4096], P('dp', None, 'mp'), may hold values from -45 to 45
- reward_hidden: bfloat16 [2048, 7, 4096], P('dp', None, 'mp'), may hold values from -140 to 140
- head_weight: bfloat16 [4096, 65536], P('mp', 'dp'), may hold values from -0.25 to 0.25
- norm_gain: float32 [4096], P('mp'), may hold values from 0.1 to 1.9
- score_weight: float32 [4096], P('mp'), may hold values from -0.09375 to 0.09375
- value_weight: float32 [4096], P('mp'), may hold values from -0.09375 to 0.09375
- old_logprob: float32 [8192], P('dp'), may hold values from -14 to -1
Outputs:
- ref_logprob: float32 [8192], P('dp')
- advantage: float32 [8192], P('dp')
The draws below stay inside these ranges and needn't reach their ends.
Inputs may be any that keep to these rules, and one draw needn't show every extreme that they name: `pack_dest`: request i belongs to request shard i // 64. Each request shard sends exactly 2 of its requests to every packed shard. A packed shard lists its requests by request shard, then by request index, and packs their tokens in that order from slot 0. In that order the requests of a packed shard form pairs whose lengths sum to 8, so every packed shard holds exactly 256 tokens; every packed shard has a request of length 1 and one of length 7.
All inputs are finite; a program needn't handle non-finite values.
Results may differ from the reference program's by a relative error of at most 0.0003.
Values may be sent and summed in bfloat16 or wider, within the bound.
No kernel may reach another device: no remote copies, remote signals or barrier semaphores. Data moves between devices by JAX's collectives and lax.ppermute only.
A program may use at most 192 MiB of HBM per device.

```python
import math
import jax
import jax.numpy as jnp
import numpy as np
from jax import lax

D = 4096
VOCAB = 65536
MAXLEN = 7
REQ_DEV = 64
PROMPTS = 2048
SLOT_DEV = 256
TOKENS = 8192


def routing_tables(key):
    shards = PROMPTS // REQ_DEV
    per_pair = REQ_DEV // shards
    source_keys = jax.random.split(jax.random.fold_in(key, 101), shards)
    orders = jax.vmap(lambda sub_key: jax.random.permutation(sub_key, REQ_DEV))(source_keys)
    target_shard = (jnp.arange(shards, dtype=jnp.int32)[:, None] + orders.astype(jnp.int32)) % shards
    same_shard = target_shard[:, :, None] == target_shard[:, None, :]
    earlier = jnp.arange(REQ_DEV)[None, :] < jnp.arange(REQ_DEV)[:, None]
    rank_in = jnp.sum(jnp.logical_and(same_shard, earlier[None]).astype(jnp.int32), axis=2).astype(jnp.int32)
    packed_pos = jnp.arange(shards, dtype=jnp.int32)[:, None] * per_pair + rank_in
    pair_count = REQ_DEV // 2
    first_len = jax.random.randint(jax.random.fold_in(key, 102), (shards, pair_count), 1, MAXLEN + 1)
    chosen = jax.random.randint(jax.random.fold_in(key, 103), (shards,), 0, pair_count)
    first_len = jnp.where(jnp.arange(pair_count)[None, :] == chosen[:, None], 1, first_len)
    packed = jnp.stack([first_len, MAXLEN + 1 - first_len], axis=2).reshape(shards * REQ_DEV).astype(jnp.int32)
    length = packed[(target_shard * REQ_DEV + packed_pos).reshape(-1)]
    return (target_shard.reshape(-1).astype(jnp.int32), length.astype(jnp.int32))


def draw_pack_dest(key, part):
    return routing_tables(key)[0]


def draw_lengths(key, part):
    return routing_tables(key)[1]


def draw_ref_hidden(key, part):
    full_shape = (PROMPTS, MAXLEN, D)
    values = jnp.clip(jax.random.normal(key, full_shape, jnp.float32), -6.0, 6.0)
    return values.astype(jnp.bfloat16)


def draw_reward_hidden(key, part):
    full_shape = (PROMPTS, MAXLEN, D)
    column = jnp.exp(math.log(10.0) * jnp.arange(D, dtype=jnp.float32) / D)
    values = jnp.clip(jax.random.normal(key, full_shape, jnp.float32), -6.0, 6.0) * column
    return values.astype(jnp.bfloat16)


def place_ends(entries, own_key, least, top_value):
    index_at = [jax.random.randint(jax.random.fold_in(own_key, axis), (), 0, length) for axis, length in enumerate(entries.shape)]
    main_axis = entries.shape.index(max(entries.shape))
    next_to = index_at[:main_axis] + [(index_at[main_axis] + 1) % entries.shape[main_axis]] + index_at[main_axis + 1:]
    return entries.at[tuple(index_at)].set(least).at[tuple(next_to)].set(top_value)


def level_of(stream_key, extent, cuts, low, high):
    loudness = 1.0
    for dim, blocks in cuts:
        heights = jax.random.uniform(jax.random.fold_in(jax.random.fold_in(stream_key, 6), dim), (blocks,), jnp.float32, low / len(cuts), high / len(cuts))
        loudness = loudness * jnp.repeat(jnp.exp(heights), extent[dim] // blocks).reshape((-1,) + (1,) * (len(extent) - 1 - dim))
    return loudness


def cumulative_ranks(count, slope):
    portions = [(1 << 20) // math.isqrt(standing ** slope) + 1 for standing in range(1, count + 1)]
    width = 1 + sum(portions) // (1 << 30)
    return np.cumsum(np.array([max(1, weight // width) for weight in portions]))


def skewed_ids(stream_key, extent, count, lean):
    listing = cumulative_ranks(count, lean)
    ticket = jax.random.randint(jax.random.fold_in(stream_key, 1), extent, 0, int(listing[count - 1]))
    standing = jnp.searchsorted(jnp.asarray(listing, jnp.int32), ticket, side="right")
    return jax.random.permutation(jax.random.fold_in(stream_key, 2), count)[standing].astype(jnp.int32)


def bell_draw(stream_key, shape, deviation, reach, cuts=(), kind=jnp.bfloat16):
    level = level_of(stream_key, shape, cuts, -0.22, 0.18) if cuts else 1.0
    array = jax.random.normal(stream_key, shape, jnp.float32) * deviation * level
    return jnp.minimum(jnp.maximum(array, -reach), reach).astype(kind)


def setup_inputs(seed: int = 0) -> dict:
    keys = jax.random.split(jax.random.key(seed), 11)
    return {
        "token_ids": place_ends(skewed_ids(keys[0], (PROMPTS, MAXLEN), VOCAB, 2), jax.random.fold_in(keys[0], 3), 0, VOCAB - 1).astype(jnp.int32),
        "lengths": draw_lengths(jax.random.fold_in(keys[10], 71), 0),
        "pack_dest": draw_pack_dest(jax.random.fold_in(keys[10], 71), 0),
        "ref_hidden": draw_ref_hidden(jax.random.fold_in(keys[10], 71), 0),
        "reward_hidden": draw_reward_hidden(jax.random.fold_in(keys[10], 71), 0),
        "head_weight": bell_draw(keys[5], (D, VOCAB), (D // 9) ** -0.5, 0.25, ((0, 8), (1, 32))),
        "norm_gain": jnp.clip(1.0 + 0.18 * jax.random.normal(keys[6], (D,), jnp.float32), 0.1, 1.9),
        "score_weight": bell_draw(keys[7], (D,), D ** -0.5, 0.09375, ((0, 8),), jnp.float32),
        "value_weight": bell_draw(keys[8], (D,), D ** -0.5, 0.09375, ((0, 8),), jnp.float32),
        "old_logprob": jnp.clip(-14.0 + 13.0 * jax.random.uniform(keys[9], (TOKENS,), jnp.float32) ** level_of(keys[9], (TOKENS,), ((0, 32),), -0.2, 0.2), -14.0, -1.0),
    }


kl_coef = 0.1
discount = 0.99
gae_mix = 0.95
norm_eps = 1e-05

def pack_tables(pack_dest, lengths, shards, req_dev, max_len, slot_dev):
    per_pair = req_dev // shards
    target_shard = pack_dest.reshape(shards, req_dev)
    same_shard = target_shard[:, :, None] == target_shard[:, None, :]
    earlier = jnp.arange(req_dev, dtype=jnp.int32)[None, :] < jnp.arange(req_dev, dtype=jnp.int32)[:, None]
    rank_in = lax.optimization_barrier(jnp.sum(jnp.logical_and(same_shard, earlier[None]).astype(jnp.int32), axis=2)).astype(jnp.int32)
    packed_pos = (jnp.arange(shards, dtype=jnp.int32)[:, None] * per_pair + rank_in).astype(jnp.int32)
    packed_place = (target_shard * req_dev + packed_pos).reshape(-1).astype(jnp.int32)
    source_of = jnp.zeros((shards * req_dev,), jnp.int32).at[packed_place].set(jnp.arange(shards * req_dev, dtype=jnp.int32)).reshape(shards, req_dev)
    packed_len = lengths[source_of].astype(jnp.int32)
    offsets = (jnp.cumsum(packed_len, axis=1, dtype=jnp.int32) - packed_len).astype(jnp.int32)
    slot_ids = jnp.arange(slot_dev, dtype=jnp.int32)
    request_at = (lax.optimization_barrier(jnp.sum((offsets[:, None, :] <= slot_ids[None, :, None]).astype(jnp.int32), axis=2)) - 1).astype(jnp.int32)
    start_at = jnp.take_along_axis(offsets, request_at, axis=1)
    offset_in = (slot_ids[None, :] - start_at).astype(jnp.int32)
    is_last = offset_in == jnp.take_along_axis(packed_len, request_at, axis=1) - 1
    source_prompt = jnp.take_along_axis(source_of, request_at, axis=1)
    return (target_shard, packed_pos, request_at, offset_in, is_last, source_prompt)

def advantages(reward, value_est, is_last, request_at):
    slot_count = reward.shape[0]
    next_value = jnp.concatenate([value_est[1:], jnp.zeros((1,), jnp.float32)])
    not_last = 1.0 - is_last.astype(jnp.float32)
    td_error = reward + discount * next_value * not_last - value_est
    slot_ids = jnp.arange(slot_count, dtype=jnp.int32)
    step_gap = (slot_ids[None, :] - slot_ids[:, None]).astype(jnp.float32)
    same_req = jnp.logical_and(request_at[:, None] == request_at[None, :], step_gap >= 0)
    weights = jnp.where(same_req, jnp.exp(jnp.maximum(step_gap, 0.0) * math.log(discount * gae_mix)), 0.0)
    return jnp.dot(weights, td_error, precision=lax.Precision.HIGHEST)

def reference(token_ids, lengths, pack_dest, ref_hidden, reward_hidden, head_weight, norm_gain, score_weight, value_weight, old_logprob):
    shards = PROMPTS // REQ_DEV
    target_shard, packed_pos, request_at, offset_in, is_last, source_prompt = pack_tables(pack_dest, lengths, shards, REQ_DEV, MAXLEN, SLOT_DEV)
    flat_rows = (source_prompt * MAXLEN + offset_in).reshape(-1).astype(jnp.int32)
    ref_rows = ref_hidden.reshape(PROMPTS * MAXLEN, D)[flat_rows]
    reward_rows = reward_hidden.reshape(PROMPTS * MAXLEN, D)[flat_rows]
    targets = token_ids.reshape(-1)[flat_rows]
    block_rows = math.gcd(TOKENS, 256)

    def score_block(inputs):
        row_block, id_block = inputs
        logits = jnp.dot(row_block, head_weight, preferred_element_type=jnp.float32)
        row_max = lax.optimization_barrier(jnp.max(logits, axis=1))
        exp_total = lax.optimization_barrier(jnp.sum(jnp.exp(logits - row_max[:, None]), axis=1))
        target_logit = jnp.take_along_axis(logits, id_block[:, None], axis=1)[:, 0]
        return target_logit - row_max - jnp.log(exp_total)
    ref_logprob = lax.map(score_block, (ref_rows.reshape(-1, block_rows, D), targets.reshape(-1, block_rows))).reshape(-1)
    hidden_f = reward_rows.astype(jnp.float32)
    squares = lax.optimization_barrier(jnp.sum(hidden_f * hidden_f, axis=1))
    score_dot = lax.optimization_barrier(jnp.sum(hidden_f * (norm_gain * score_weight), axis=1))
    value_dot = lax.optimization_barrier(jnp.sum(hidden_f * (norm_gain * value_weight), axis=1))
    inv_rms = lax.rsqrt(squares / D + norm_eps)
    score = (score_dot * inv_rms).reshape(shards, SLOT_DEV)
    value_est = (value_dot * inv_rms).reshape(shards, SLOT_DEV)
    reward = -kl_coef * (old_logprob.reshape(shards, SLOT_DEV) - ref_logprob.reshape(shards, SLOT_DEV)) + jnp.where(is_last, score, 0.0)
    advantage = jax.vmap(advantages)(reward, value_est, is_last, request_at)
    return (ref_logprob, advantage.reshape(-1))
```

```python
import jax
import jax.numpy as jnp
from jax import lax
from jax.sharding import PartitionSpec as P

kl_coef = 0.1
discount = 0.99
gae_mix = 0.95
norm_eps = 1e-05


def pair_rank(dest):
    count = dest.shape[-1]
    idx = jnp.arange(count, dtype=jnp.int32)
    same = dest[..., None, :] == dest[..., :, None]
    earlier = idx[None, :] < idx[:, None]
    return jnp.sum(jnp.logical_and(same, earlier).astype(jnp.int32), axis=-1)


def body(
    token_ids,
    lengths,
    pack_dest,
    ref_hidden,
    reward_hidden,
    head_weight,
    norm_gain,
    score_weight,
    value_weight,
    old_logprob,
):
    shards = lax.axis_size("dp")
    ways = lax.axis_size("mp")
    me = lax.axis_index("dp")
    part = lax.axis_index("mp")
    req_dev, max_len, width_dev = ref_hidden.shape
    pair_len = max_len + 1
    slot_dev = shards * pair_len
    sub_len = slot_dev // ways
    blocks = sub_len // pair_len
    width_full = width_dev * ways
    steps = jnp.arange(max_len, dtype=jnp.int32)

    dest = lax.dynamic_slice_in_dim(pack_dest, me * req_dev, req_dev)
    size = lax.dynamic_slice_in_dim(lengths, me * req_dev, req_dev)
    rank = pair_rank(dest)
    row = dest[:, None] * pair_len + steps[None, :] + rank[:, None] * (pair_len - size[:, None])
    row = jnp.where(steps[None, :] < size[:, None], row, -1).reshape(-1)
    onehot = (row[None, :] == jnp.arange(slot_dev, dtype=jnp.int32)[:, None]).astype(jnp.bfloat16)
    ref_send = jnp.dot(
        onehot, ref_hidden.reshape(req_dev * max_len, width_dev), preferred_element_type=jnp.float32
    ).astype(jnp.bfloat16)
    reward_send = jnp.dot(
        onehot, reward_hidden.reshape(req_dev * max_len, width_dev), preferred_element_type=jnp.float32
    ).astype(jnp.bfloat16)
    send = jnp.concatenate([ref_send, reward_send], axis=1).reshape(shards, pair_len, 2 * width_dev)
    got = lax.all_to_all(send, "dp", 0, 0, tiled=True).reshape(slot_dev, 2 * width_dev)
    ref_packed = got[:, :width_dev]
    reward_packed = got[:, width_dev:]

    own_rows = lax.all_to_all(
        ref_packed.reshape(ways, sub_len, width_dev), "mp", 0, 2, tiled=True
    ).reshape(sub_len, width_full)
    block_rows = lax.all_gather(own_rows, "dp", axis=0, tiled=True)
    weight = lax.all_gather(head_weight, "mp", axis=0, tiled=True)

    first_src = part * blocks
    dest4 = lax.dynamic_slice_in_dim(pack_dest, first_src * req_dev, blocks * req_dev).reshape(
        blocks, req_dev
    )
    size4 = lax.dynamic_slice_in_dim(lengths, first_src * req_dev, blocks * req_dev).reshape(
        blocks, req_dev
    )
    tok4 = lax.dynamic_slice_in_dim(token_ids, first_src * req_dev, blocks * req_dev, axis=0)
    rank4 = pair_rank(dest4)
    key = (
        dest4[:, :, None] * sub_len
        + jnp.arange(blocks, dtype=jnp.int32)[:, None, None] * pair_len
        + steps[None, None, :]
        + rank4[:, :, None] * (pair_len - size4[:, :, None])
    )
    key = jnp.where(steps[None, None, :] < size4[:, :, None], key, -1).reshape(-1)
    hits = key[None, :] == jnp.arange(shards * sub_len, dtype=jnp.int32)[:, None]
    targets = jnp.sum(jnp.where(hits, tok4.reshape(-1)[None, :], 0), axis=1)

    logits = jnp.dot(block_rows, weight, preferred_element_type=jnp.float32)
    vocab_dev = head_weight.shape[1]
    row_max = jnp.max(logits, axis=1)
    exp_total = jnp.sum(jnp.exp(logits - row_max[:, None]), axis=1)
    column = jnp.arange(vocab_dev, dtype=jnp.int32)[None, :] + me * vocab_dev
    target_logit = jnp.sum(jnp.where(column == targets[:, None], logits, 0.0), axis=1)
    stats = jnp.stack([row_max, exp_total, target_logit]).reshape(3, shards, sub_len)
    stats = lax.all_to_all(stats, "dp", 1, 1, tiled=True)
    joint_max = jnp.max(stats[0], axis=0)
    joint_total = jnp.sum(stats[1] * jnp.exp(stats[0] - joint_max[None, :]), axis=0)
    joint_target = jnp.sum(stats[2], axis=0)
    block_logprob = joint_target - joint_max - jnp.log(joint_total)
    ref_logprob = lax.all_gather(block_logprob, "mp", axis=0, tiled=True)

    hidden_f = reward_packed.astype(jnp.float32)
    sums = jnp.stack(
        [
            jnp.sum(hidden_f * hidden_f, axis=1),
            jnp.sum(hidden_f * (norm_gain * score_weight), axis=1),
            jnp.sum(hidden_f * (norm_gain * value_weight), axis=1),
        ]
    )
    squares, score_dot, value_dot = lax.psum(sums, "mp")
    inv_rms = lax.rsqrt(squares / width_full + norm_eps)
    score = score_dot * inv_rms
    value_est = value_dot * inv_rms

    mine = (pack_dest.reshape(shards, req_dev) == me).astype(jnp.int32)
    is_first = jnp.logical_and(mine == 1, jnp.cumsum(mine, axis=1) == 1)
    first_len = jnp.sum(jnp.where(is_first, lengths.reshape(shards, req_dev), 0), axis=1)
    place = jnp.arange(pair_len, dtype=jnp.int32)[None, :]
    is_last = jnp.logical_or(place == first_len[:, None] - 1, place == pair_len - 1)
    is_last_flat = is_last.reshape(-1)

    reward = -kl_coef * (old_logprob - ref_logprob) + jnp.where(is_last_flat, score, 0.0)
    next_value = jnp.concatenate([value_est[1:], jnp.zeros((1,), jnp.float32)])
    not_last = 1.0 - is_last_flat.astype(jnp.float32)
    td_error = (reward + discount * next_value * not_last - value_est).reshape(shards, pair_len)
    decay = discount * gae_mix
    carry = td_error[:, pair_len - 1]
    columns = [carry]
    for step in range(pair_len - 2, -1, -1):
        carry = td_error[:, step] + decay * jnp.where(is_last[:, step], 0.0, carry)
        columns.append(carry)
    advantage = jnp.stack(columns[::-1], axis=1).reshape(-1)
    return (ref_logprob, advantage)


def solution(mesh):
    return jax.shard_map(
        body,
        mesh=mesh,
        in_specs=(
            P(),
            P(),
            P(),
            P("dp", None, "mp"),
            P("dp", None, "mp"),
            P("mp", "dp"),
            P("mp"),
            P("mp"),
            P("mp"),
            P("dp"),
        ),
        out_specs=(P("dp"), P("dp")),
        check_vma=False,
    )
```

```python
import jax
import jax.numpy as jnp
from jax import lax
from jax.sharding import PartitionSpec as P

kl_coef = 0.1
discount = 0.99
gae_mix = 0.95
norm_eps = 1e-05


def pair_rank(dest):
    count = dest.shape[-1]
    idx = jnp.arange(count, dtype=jnp.int32)
    same = dest[..., None, :] == dest[..., :, None]
    earlier = idx[None, :] < idx[:, None]
    return jnp.sum(jnp.logical_and(same, earlier).astype(jnp.int32), axis=-1)


def body(
    token_ids,
    lengths,
    pack_dest,
    ref_hidden,
    reward_hidden,
    head_weight,
    norm_gain,
    score_weight,
    value_weight,
    old_logprob,
):
    shards = lax.axis_size("dp")
    ways = lax.axis_size("mp")
    me = lax.axis_index("dp")
    part = lax.axis_index("mp")
    req_dev, max_len, width_dev = ref_hidden.shape
    pair_len = max_len + 1
    slot_dev = shards * pair_len
    sub_len = slot_dev // ways
    blocks = sub_len // pair_len
    width_full = width_dev * ways
    steps = jnp.arange(max_len, dtype=jnp.int32)

    dest = lax.dynamic_slice_in_dim(pack_dest, me * req_dev, req_dev)
    size = lax.dynamic_slice_in_dim(lengths, me * req_dev, req_dev)
    rank = pair_rank(dest)
    row = dest[:, None] * pair_len + steps[None, :] + rank[:, None] * (pair_len - size[:, None])
    row = jnp.where(steps[None, :] < size[:, None], row, -1).reshape(-1)
    onehot = (row[None, :] == jnp.arange(slot_dev, dtype=jnp.int32)[:, None]).astype(jnp.bfloat16)
    ref_send = jnp.dot(
        onehot, ref_hidden.reshape(req_dev * max_len, width_dev), preferred_element_type=jnp.float32
    ).astype(jnp.bfloat16)
    reward_send = jnp.dot(
        onehot, reward_hidden.reshape(req_dev * max_len, width_dev), preferred_element_type=jnp.float32
    ).astype(jnp.bfloat16)
    send = jnp.concatenate([ref_send, reward_send], axis=1).reshape(shards, pair_len, 2 * width_dev)
    got = lax.all_to_all(send, "dp", 0, 0, tiled=True).reshape(slot_dev, 2 * width_dev)
    ref_packed = got[:, :width_dev]
    reward_packed = got[:, width_dev:]

    chips = ways // 2
    own_core = [head_weight] + [
        lax.ppermute(head_weight, "mp", [(i, (i + 2 * shift) % ways) for i in range(ways)])
        for shift in range(1, chips)
    ]
    mate_core = [lax.ppermute(block, "mp", [(i, i ^ 1) for i in range(ways)]) for block in own_core]
    weight = jnp.concatenate(own_core + mate_core, axis=0)
    chip, core = part // 2, part % 2
    order = jnp.arange(ways, dtype=jnp.int32)
    source_chip = (chip - order % chips) % chips
    source_core = jnp.where(order < chips, core, 1 - core)
    pick = (
        (source_chip * 2 + source_core)[:, None] == jnp.arange(ways, dtype=jnp.int32)[None, :]
    ).astype(jnp.bfloat16)

    parts_rows = lax.all_to_all(
        ref_packed.reshape(ways, sub_len, width_dev), "mp", 0, 0, tiled=True
    )
    own_rows = jnp.einsum(
        "msf,nm->snf", parts_rows, pick, preferred_element_type=jnp.float32
    ).astype(jnp.bfloat16).reshape(sub_len, width_full)
    block_rows = lax.all_gather(own_rows, "dp", axis=0, tiled=True)

    first_src = part * blocks
    dest4 = lax.dynamic_slice_in_dim(pack_dest, first_src * req_dev, blocks * req_dev).reshape(
        blocks, req_dev
    )
    size4 = lax.dynamic_slice_in_dim(lengths, first_src * req_dev, blocks * req_dev).reshape(
        blocks, req_dev
    )
    tok4 = lax.dynamic_slice_in_dim(token_ids, first_src * req_dev, blocks * req_dev, axis=0)
    rank4 = pair_rank(dest4)
    key = (
        dest4[:, :, None] * sub_len
        + jnp.arange(blocks, dtype=jnp.int32)[:, None, None] * pair_len
        + steps[None, None, :]
        + rank4[:, :, None] * (pair_len - size4[:, :, None])
    )
    key = jnp.where(steps[None, None, :] < size4[:, :, None], key, -1).reshape(-1)
    hits = key[None, :] == jnp.arange(shards * sub_len, dtype=jnp.int32)[:, None]
    targets = jnp.sum(jnp.where(hits, tok4.reshape(-1)[None, :], 0), axis=1)

    logits = jnp.dot(block_rows, weight, preferred_element_type=jnp.float32)
    vocab_dev = head_weight.shape[1]
    row_max = jnp.max(logits, axis=1)
    exp_total = jnp.sum(jnp.exp(logits - row_max[:, None]), axis=1)
    column = jnp.arange(vocab_dev, dtype=jnp.int32)[None, :] + me * vocab_dev
    target_logit = jnp.sum(jnp.where(column == targets[:, None], logits, 0.0), axis=1)
    stats = jnp.stack([row_max, exp_total, target_logit]).reshape(3, shards, sub_len)
    stats = lax.all_to_all(stats, "dp", 1, 1, tiled=True)
    joint_max = jnp.max(stats[0], axis=0)
    joint_total = jnp.sum(stats[1] * jnp.exp(stats[0] - joint_max[None, :]), axis=0)
    joint_target = jnp.sum(stats[2], axis=0)
    block_logprob = joint_target - joint_max - jnp.log(joint_total)
    ref_logprob = lax.all_gather(block_logprob, "mp", axis=0, tiled=True)

    hidden_f = reward_packed.astype(jnp.float32)
    sums = jnp.stack(
        [
            jnp.sum(hidden_f * hidden_f, axis=1),
            jnp.sum(hidden_f * (norm_gain * score_weight), axis=1),
            jnp.sum(hidden_f * (norm_gain * value_weight), axis=1),
        ]
    )
    squares, score_dot, value_dot = lax.psum(sums, "mp")
    inv_rms = lax.rsqrt(squares / width_full + norm_eps)
    score = score_dot * inv_rms
    value_est = value_dot * inv_rms

    mine = (pack_dest.reshape(shards, req_dev) == me).astype(jnp.int32)
    is_first = jnp.logical_and(mine == 1, jnp.cumsum(mine, axis=1) == 1)
    first_len = jnp.sum(jnp.where(is_first, lengths.reshape(shards, req_dev), 0), axis=1)
    place = jnp.arange(pair_len, dtype=jnp.int32)[None, :]
    is_last = jnp.logical_or(place == first_len[:, None] - 1, place == pair_len - 1)
    is_last_flat = is_last.reshape(-1)

    reward = -kl_coef * (old_logprob - ref_logprob) + jnp.where(is_last_flat, score, 0.0)
    next_value = jnp.concatenate([value_est[1:], jnp.zeros((1,), jnp.float32)])
    not_last = 1.0 - is_last_flat.astype(jnp.float32)
    td_error = (reward + discount * next_value * not_last - value_est).reshape(shards, pair_len)
    decay = discount * gae_mix
    carry = td_error[:, pair_len - 1]
    columns = [carry]
    for step in range(pair_len - 2, -1, -1):
        carry = td_error[:, step] + decay * jnp.where(is_last[:, step], 0.0, carry)
        columns.append(carry)
    advantage = jnp.stack(columns[::-1], axis=1).reshape(-1)
    return (ref_logprob, advantage)


def solution(mesh):
    return jax.shard_map(
        body,
        mesh=mesh,
        in_specs=(
            P(),
            P(),
            P(),
            P("dp", None, "mp"),
            P("dp", None, "mp"),
            P("mp", "dp"),
            P("mp"),
            P("mp"),
            P("mp"),
            P("dp"),
        ),
        out_specs=(P("dp"), P("dp")),
        check_vma=False,
    )
```

```python
import jax
import jax.numpy as jnp
from jax import lax
from jax.experimental import pallas as pl
from jax.experimental.pallas import tpu as pltpu
from jax.sharding import PartitionSpec as P

kl_coef = 0.1
discount = 0.99
gae_mix = 0.95
norm_eps = 1e-05


def pair_rank(dest):
    count = dest.shape[-1]
    idx = jnp.arange(count, dtype=jnp.int32)
    same = dest[..., None, :] == dest[..., :, None]
    earlier = idx[None, :] < idx[:, None]
    return jnp.sum(jnp.logical_and(same, earlier).astype(jnp.int32), axis=-1)


def stats_kernel(pieces, tile_n, target_ref, rows_ref, *refs):
    weight_refs = refs[:pieces]
    max_ref, total_ref, target_logit_ref = refs[pieces:]
    width = weight_refs[0].shape[0]
    logits = jnp.dot(rows_ref[:, 0:width], weight_refs[0][...], preferred_element_type=jnp.float32)
    for k in range(1, pieces):
        logits = logits + jnp.dot(
            rows_ref[:, k * width : (k + 1) * width],
            weight_refs[k][...],
            preferred_element_type=jnp.float32,
        )
    row_max = jnp.max(logits, axis=1, keepdims=True)
    total = jnp.sum(jnp.exp(logits - row_max), axis=1, keepdims=True)
    column = lax.broadcasted_iota(jnp.int32, logits.shape, 1) + pl.program_id(0) * tile_n
    target_logit = jnp.sum(jnp.where(column == target_ref[...], logits, 0.0), axis=1, keepdims=True)
    max_ref[0] = row_max
    total_ref[0] = total
    target_logit_ref[0] = target_logit


def logit_stats(rows, pieces, local_target, tile_m=256, tile_n=1024):
    count, width_full = rows.shape
    width, vocab = pieces[0].shape
    grid = (vocab // tile_n, count // tile_m)
    stat_shape = jax.ShapeDtypeStruct((grid[0], count, 1), jnp.float32)
    stat_spec = pl.BlockSpec((1, tile_m, 1), lambda j, i: (j, i, 0))
    return pl.pallas_call(
        lambda *refs: stats_kernel(len(pieces), tile_n, *refs),
        grid=grid,
        in_specs=[
            pl.BlockSpec((tile_m, 1), lambda j, i: (i, 0)),
            pl.BlockSpec((tile_m, width_full), lambda j, i: (i, 0)),
        ]
        + [pl.BlockSpec((width, tile_n), lambda j, i: (0, j)) for _ in pieces],
        out_specs=[stat_spec, stat_spec, stat_spec],
        out_shape=[stat_shape, stat_shape, stat_shape],
        compiler_params=pltpu.CompilerParams(vmem_limit_bytes=48 * 1024 * 1024),
        cost_estimate=pl.CostEstimate(
            flops=2 * count * width_full * vocab,
            transcendentals=count * vocab,
            bytes_accessed=2 * width_full * vocab + 2 * count * width_full * grid[0],
        ),
    )(local_target.reshape(count, 1), rows, *pieces)


def body(
    token_ids,
    lengths,
    pack_dest,
    ref_hidden,
    reward_hidden,
    head_weight,
    norm_gain,
    score_weight,
    value_weight,
    old_logprob,
):
    shards = lax.axis_size("dp")
    ways = lax.axis_size("mp")
    me = lax.axis_index("dp")
    part = lax.axis_index("mp")
    req_dev, max_len, width_dev = ref_hidden.shape
    pair_len = max_len + 1
    slot_dev = shards * pair_len
    sub_len = slot_dev // ways
    blocks = sub_len // pair_len
    width_full = width_dev * ways
    steps = jnp.arange(max_len, dtype=jnp.int32)

    dest = lax.dynamic_slice_in_dim(pack_dest, me * req_dev, req_dev)
    size = lax.dynamic_slice_in_dim(lengths, me * req_dev, req_dev)
    rank = pair_rank(dest)
    row = dest[:, None] * pair_len + steps[None, :] + rank[:, None] * (pair_len - size[:, None])
    row = jnp.where(steps[None, :] < size[:, None], row, -1).reshape(-1)
    onehot = (row[None, :] == jnp.arange(slot_dev, dtype=jnp.int32)[:, None]).astype(jnp.bfloat16)
    ref_send = jnp.dot(
        onehot, ref_hidden.reshape(req_dev * max_len, width_dev), preferred_element_type=jnp.float32
    ).astype(jnp.bfloat16)
    reward_send = jnp.dot(
        onehot, reward_hidden.reshape(req_dev * max_len, width_dev), preferred_element_type=jnp.float32
    ).astype(jnp.bfloat16)
    send = jnp.concatenate([ref_send, reward_send], axis=1).reshape(shards, pair_len, 2 * width_dev)
    got = lax.all_to_all(send, "dp", 0, 0, tiled=True).reshape(slot_dev, 2 * width_dev)
    ref_packed = got[:, :width_dev]
    reward_packed = got[:, width_dev:]

    chips = ways // 2
    own_core = [head_weight] + [
        lax.ppermute(head_weight, "mp", [(i, (i + 2 * shift) % ways) for i in range(ways)])
        for shift in range(1, chips)
    ]
    mate_core = [lax.ppermute(block, "mp", [(i, i ^ 1) for i in range(ways)]) for block in own_core]
    chip, core = part // 2, part % 2
    order = jnp.arange(ways, dtype=jnp.int32)
    source_chip = (chip - order % chips) % chips
    source_core = jnp.where(order < chips, core, 1 - core)
    pick = (
        (source_chip * 2 + source_core)[:, None] == jnp.arange(ways, dtype=jnp.int32)[None, :]
    ).astype(jnp.bfloat16)

    parts_rows = lax.all_to_all(
        ref_packed.reshape(ways, sub_len, width_dev), "mp", 0, 0, tiled=True
    )
    own_rows = jnp.einsum(
        "msf,nm->snf", parts_rows, pick, preferred_element_type=jnp.float32
    ).astype(jnp.bfloat16).reshape(sub_len, width_full)
    block_rows = lax.all_gather(own_rows, "dp", axis=0, tiled=True)

    first_src = part * blocks
    dest4 = lax.dynamic_slice_in_dim(pack_dest, first_src * req_dev, blocks * req_dev).reshape(
        blocks, req_dev
    )
    size4 = lax.dynamic_slice_in_dim(lengths, first_src * req_dev, blocks * req_dev).reshape(
        blocks, req_dev
    )
    tok4 = lax.dynamic_slice_in_dim(token_ids, first_src * req_dev, blocks * req_dev, axis=0)
    rank4 = pair_rank(dest4)
    key = (
        dest4[:, :, None] * sub_len
        + jnp.arange(blocks, dtype=jnp.int32)[:, None, None] * pair_len
        + steps[None, None, :]
        + rank4[:, :, None] * (pair_len - size4[:, :, None])
    )
    key = jnp.where(steps[None, None, :] < size4[:, :, None], key, -1).reshape(-1)
    hits = key[None, :] == jnp.arange(shards * sub_len, dtype=jnp.int32)[:, None]
    targets = jnp.sum(jnp.where(hits, tok4.reshape(-1)[None, :], 0), axis=1)

    vocab_dev = head_weight.shape[1]
    tile_max, tile_total, tile_target = logit_stats(
        block_rows, own_core + mate_core, targets - me * vocab_dev
    )
    row_max = jnp.max(tile_max[:, :, 0], axis=0)
    exp_total = jnp.sum(tile_total[:, :, 0] * jnp.exp(tile_max[:, :, 0] - row_max[None, :]), axis=0)
    target_logit = jnp.sum(tile_target[:, :, 0], axis=0)
    stats = jnp.stack([row_max, exp_total, target_logit]).reshape(3, shards, sub_len)
    stats = lax.all_to_all(stats, "dp", 1, 1, tiled=True)
    joint_max = jnp.max(stats[0], axis=0)
    joint_total = jnp.sum(stats[1] * jnp.exp(stats[0] - joint_max[None, :]), axis=0)
    joint_target = jnp.sum(stats[2], axis=0)
    block_logprob = joint_target - joint_max - jnp.log(joint_total)
    ref_logprob = lax.all_gather(block_logprob, "mp", axis=0, tiled=True)

    hidden_f = reward_packed.astype(jnp.float32)
    sums = jnp.stack(
        [
            jnp.sum(hidden_f * hidden_f, axis=1),
            jnp.sum(hidden_f * (norm_gain * score_weight), axis=1),
            jnp.sum(hidden_f * (norm_gain * value_weight), axis=1),
        ]
    )
    squares, score_dot, value_dot = lax.psum(sums, "mp")
    inv_rms = lax.rsqrt(squares / width_full + norm_eps)
    score = score_dot * inv_rms
    value_est = value_dot * inv_rms

    mine = (pack_dest.reshape(shards, req_dev) == me).astype(jnp.int32)
    is_first = jnp.logical_and(mine == 1, jnp.cumsum(mine, axis=1) == 1)
    first_len = jnp.sum(jnp.where(is_first, lengths.reshape(shards, req_dev), 0), axis=1)
    place = jnp.arange(pair_len, dtype=jnp.int32)[None, :]
    is_last = jnp.logical_or(place == first_len[:, None] - 1, place == pair_len - 1)
    is_last_flat = is_last.reshape(-1)

    reward = -kl_coef * (old_logprob - ref_logprob) + jnp.where(is_last_flat, score, 0.0)
    next_value = jnp.concatenate([value_est[1:], jnp.zeros((1,), jnp.float32)])
    not_last = 1.0 - is_last_flat.astype(jnp.float32)
    td_error = (reward + discount * next_value * not_last - value_est).reshape(shards, pair_len)
    decay = discount * gae_mix
    carry = td_error[:, pair_len - 1]
    columns = [carry]
    for step in range(pair_len - 2, -1, -1):
        carry = td_error[:, step] + decay * jnp.where(is_last[:, step], 0.0, carry)
        columns.append(carry)
    advantage = jnp.stack(columns[::-1], axis=1).reshape(-1)
    return (ref_logprob, advantage)


def solution(mesh):
    return jax.shard_map(
        body,
        mesh=mesh,
        in_specs=(
            P(),
            P(),
            P(),
            P("dp", None, "mp"),
            P("dp", None, "mp"),
            P("mp", "dp"),
            P("mp"),
            P("mp"),
            P("mp"),
            P("dp"),
        ),
        out_specs=(P("dp"), P("dp")),
        check_vma=False,
    )
```

```python
import jax
import jax.numpy as jnp
from jax import lax
from jax.experimental import pallas as pl
from jax.experimental.pallas import tpu as pltpu
from jax.sharding import PartitionSpec as P

kl_coef = 0.1
discount = 0.99
gae_mix = 0.95
norm_eps = 1e-05


def pair_rank(dest):
    count = dest.shape[-1]
    idx = jnp.arange(count, dtype=jnp.int32)
    same = dest[..., None, :] == dest[..., :, None]
    earlier = idx[None, :] < idx[:, None]
    return jnp.sum(jnp.logical_and(same, earlier).astype(jnp.int32), axis=-1)


def stats_kernel(pieces, tile_n, target_ref, rows_ref, *refs):
    weight_refs = refs[:pieces]
    max_ref, total_ref, target_logit_ref = refs[pieces:]
    width = weight_refs[0].shape[0]
    logits = jnp.dot(rows_ref[:, 0:width], weight_refs[0][...], preferred_element_type=jnp.float32)
    for k in range(1, pieces):
        logits = logits + jnp.dot(
            rows_ref[:, k * width : (k + 1) * width],
            weight_refs[k][...],
            preferred_element_type=jnp.float32,
        )
    row_max = jnp.max(logits, axis=1, keepdims=True)
    total = jnp.sum(jnp.exp(logits - row_max), axis=1, keepdims=True)
    column = lax.broadcasted_iota(jnp.int32, logits.shape, 1) + pl.program_id(0) * tile_n
    target_logit = jnp.sum(jnp.where(column == target_ref[...], logits, 0.0), axis=1, keepdims=True)
    max_ref[0] = row_max
    total_ref[0] = total
    target_logit_ref[0] = target_logit


def logit_stats(rows, pieces, local_target, tile_m=256, tile_n=1024):
    count, width_full = rows.shape
    width, vocab = pieces[0].shape
    grid = (vocab // tile_n, count // tile_m)
    stat_shape = jax.ShapeDtypeStruct((grid[0], count, 1), jnp.float32)
    stat_spec = pl.BlockSpec((1, tile_m, 1), lambda j, i: (j, i, 0))
    return pl.pallas_call(
        lambda *refs: stats_kernel(len(pieces), tile_n, *refs),
        grid=grid,
        in_specs=[
            pl.BlockSpec((tile_m, 1), lambda j, i: (i, 0)),
            pl.BlockSpec((tile_m, width_full), lambda j, i: (i, 0)),
        ]
        + [pl.BlockSpec((width, tile_n), lambda j, i: (0, j)) for _ in pieces],
        out_specs=[stat_spec, stat_spec, stat_spec],
        out_shape=[stat_shape, stat_shape, stat_shape],
        compiler_params=pltpu.CompilerParams(vmem_limit_bytes=48 * 1024 * 1024),
        cost_estimate=pl.CostEstimate(
            flops=2 * count * width_full * vocab,
            transcendentals=count * vocab,
            bytes_accessed=2 * width_full * vocab + 2 * count * width_full * grid[0],
        ),
    )(local_target.reshape(count, 1), rows, *pieces)


def body(
    token_ids,
    lengths,
    pack_dest,
    ref_hidden,
    reward_hidden,
    head_weight,
    norm_gain,
    score_weight,
    value_weight,
    old_logprob,
):
    shards = lax.axis_size("dp")
    ways = lax.axis_size("mp")
    me = lax.axis_index("dp")
    part = lax.axis_index("mp")
    req_dev, max_len, width_dev = ref_hidden.shape
    pair_len = max_len + 1
    slot_dev = shards * pair_len
    sub_len = slot_dev // ways
    blocks = sub_len // pair_len
    width_full = width_dev * ways
    steps = jnp.arange(max_len, dtype=jnp.int32)

    dest = lax.dynamic_slice_in_dim(pack_dest, me * req_dev, req_dev)
    size = lax.dynamic_slice_in_dim(lengths, me * req_dev, req_dev)
    rank = pair_rank(dest)
    row = dest[:, None] * pair_len + steps[None, :] + rank[:, None] * (pair_len - size[:, None])
    row = jnp.where(steps[None, :] < size[:, None], row, -1).reshape(-1)
    onehot = (row[None, :] == jnp.arange(slot_dev, dtype=jnp.int32)[:, None]).astype(jnp.bfloat16)
    ref_send = jnp.dot(
        onehot, ref_hidden.reshape(req_dev * max_len, width_dev), preferred_element_type=jnp.float32
    ).astype(jnp.bfloat16)
    reward_send = jnp.dot(
        onehot, reward_hidden.reshape(req_dev * max_len, width_dev), preferred_element_type=jnp.float32
    ).astype(jnp.bfloat16)
    reward_packed = lax.all_to_all(
        reward_send.reshape(shards, pair_len, width_dev), "dp", 0, 0, tiled=True
    ).reshape(slot_dev, width_dev)

    chips = ways // 2
    own_core = [head_weight] + [
        lax.ppermute(head_weight, "mp", [(i, (i + 2 * shift) % ways) for i in range(ways)])
        for shift in range(1, chips)
    ]
    mate_core = [lax.ppermute(block, "mp", [(i, i ^ 1) for i in range(ways)]) for block in own_core]
    chip, core = part // 2, part % 2
    order = jnp.arange(ways, dtype=jnp.int32)
    source_chip = (chip - order % chips) % chips
    source_core = jnp.where(order < chips, core, 1 - core)
    pick = (
        (source_chip * 2 + source_core)[:, None] == jnp.arange(ways, dtype=jnp.int32)[None, :]
    ).astype(jnp.bfloat16)

    parts_rows = lax.all_to_all(ref_send.reshape(ways, sub_len, width_dev), "mp", 0, 0, tiled=True)
    own_rows = jnp.einsum(
        "msf,nm->snf", parts_rows, pick, preferred_element_type=jnp.float32
    ).astype(jnp.bfloat16).reshape(sub_len, width_full)
    block_rows = lax.all_gather(own_rows, "dp", axis=0, tiled=True)

    dest_all = pack_dest.reshape(shards, req_dev)
    size_all = lengths.reshape(shards, req_dev)
    rank_all = pair_rank(dest_all)
    key = (
        dest_all[:, :, None] * pair_len
        + steps[None, None, :]
        + rank_all[:, :, None] * (pair_len - size_all[:, :, None])
        - part * sub_len
    )
    key = jnp.where(steps[None, None, :] < size_all[:, :, None], key, -1).reshape(shards, 1, -1)
    hits = key == jnp.arange(sub_len, dtype=jnp.int32)[None, :, None]
    targets = jnp.sum(
        jnp.where(hits, token_ids.reshape(shards, 1, -1), 0), axis=2
    ).reshape(-1)

    vocab_dev = head_weight.shape[1]
    tile_max, tile_total, tile_target = logit_stats(
        block_rows, own_core + mate_core, targets - me * vocab_dev
    )
    row_max = jnp.max(tile_max[:, :, 0], axis=0)
    exp_total = jnp.sum(tile_total[:, :, 0] * jnp.exp(tile_max[:, :, 0] - row_max[None, :]), axis=0)
    target_logit = jnp.sum(tile_target[:, :, 0], axis=0)
    stats = jnp.stack([row_max, exp_total, target_logit]).reshape(3, shards, blocks, pair_len)
    to_shard = jnp.arange(shards, dtype=jnp.int32)[:, None] == (
        part * blocks + jnp.arange(blocks, dtype=jnp.int32)
    )[None, :]
    routed = jnp.sum(
        jnp.where(to_shard[:, None, None, :, None], stats[None], 0.0), axis=3
    )
    routed = lax.all_to_all(routed, "dp", 0, 0, tiled=True)
    joint_max = jnp.max(routed[:, 0], axis=0)
    joint_total = jnp.sum(routed[:, 1] * jnp.exp(routed[:, 0] - joint_max[None]), axis=0)
    joint_target = jnp.sum(routed[:, 2], axis=0)
    holder = me // blocks == part
    block_logprob = jnp.where(
        holder, joint_target - joint_max - jnp.log(joint_total), 0.0
    ).reshape(-1)

    hidden_f = reward_packed.astype(jnp.float32)
    sums = jnp.stack(
        [
            jnp.sum(hidden_f * hidden_f, axis=1),
            jnp.sum(hidden_f * (norm_gain * score_weight), axis=1),
            jnp.sum(hidden_f * (norm_gain * value_weight), axis=1),
        ]
    )
    ref_logprob, squares, score_dot, value_dot = lax.psum(
        jnp.concatenate([block_logprob[None], sums]), "mp"
    )
    inv_rms = lax.rsqrt(squares / width_full + norm_eps)
    score = score_dot * inv_rms
    value_est = value_dot * inv_rms

    mine = (pack_dest.reshape(shards, req_dev) == me).astype(jnp.int32)
    is_first = jnp.logical_and(mine == 1, jnp.cumsum(mine, axis=1) == 1)
    first_len = jnp.sum(jnp.where(is_first, lengths.reshape(shards, req_dev), 0), axis=1)
    place = jnp.arange(pair_len, dtype=jnp.int32)[None, :]
    is_last = jnp.logical_or(place == first_len[:, None] - 1, place == pair_len - 1)
    is_last_flat = is_last.reshape(-1)

    reward = -kl_coef * (old_logprob - ref_logprob) + jnp.where(is_last_flat, score, 0.0)
    next_value = jnp.concatenate([value_est[1:], jnp.zeros((1,), jnp.float32)])
    not_last = 1.0 - is_last_flat.astype(jnp.float32)
    td_error = (reward + discount * next_value * not_last - value_est).reshape(shards, pair_len)
    decay = discount * gae_mix
    carry = td_error[:, pair_len - 1]
    columns = [carry]
    for step in range(pair_len - 2, -1, -1):
        carry = td_error[:, step] + decay * jnp.where(is_last[:, step], 0.0, carry)
        columns.append(carry)
    advantage = jnp.stack(columns[::-1], axis=1).reshape(-1)
    return (ref_logprob, advantage)


def solution(mesh):
    return jax.shard_map(
        body,
        mesh=mesh,
        in_specs=(
            P(),
            P(),
            P(),
            P("dp", None, "mp"),
            P("dp", None, "mp"),
            P("mp", "dp"),
            P("mp"),
            P("mp"),
            P("mp"),
            P("dp"),
        ),
        out_specs=(P("dp"), P("dp")),
        check_vma=False,
    )
```

```python
import jax
import jax.numpy as jnp
from jax import lax
from jax.experimental import pallas as pl
from jax.experimental.pallas import tpu as pltpu
from jax.sharding import PartitionSpec as P

kl_coef = 0.1
discount = 0.99
gae_mix = 0.95
norm_eps = 1e-05


def pair_rank(dest):
    count = dest.shape[-1]
    idx = jnp.arange(count, dtype=jnp.int32)
    same = dest[..., None, :] == dest[..., :, None]
    earlier = idx[None, :] < idx[:, None]
    return jnp.sum(jnp.logical_and(same, earlier).astype(jnp.int32), axis=-1)


def stats_kernel(pieces, tile_n, target_ref, rows_ref, *refs):
    weight_refs = refs[:pieces]
    max_ref, total_ref, target_logit_ref = refs[pieces:]
    width = weight_refs[0].shape[0]
    logits = jnp.dot(rows_ref[:, 0:width], weight_refs[0][...], preferred_element_type=jnp.float32)
    for k in range(1, pieces):
        logits = logits + jnp.dot(
            rows_ref[:, k * width : (k + 1) * width],
            weight_refs[k][...],
            preferred_element_type=jnp.float32,
        )
    row_max = jnp.max(logits, axis=1, keepdims=True)
    total = jnp.sum(jnp.exp(logits - row_max), axis=1, keepdims=True)
    column = lax.broadcasted_iota(jnp.int32, logits.shape, 1) + pl.program_id(0) * tile_n
    target_logit = jnp.sum(jnp.where(column == target_ref[...], logits, 0.0), axis=1, keepdims=True)
    max_ref[0] = row_max
    total_ref[0] = total
    target_logit_ref[0] = target_logit


def logit_stats(rows, pieces, local_target, tile_m=256, tile_n=1024):
    count, width_full = rows.shape
    width, vocab = pieces[0].shape
    grid = (vocab // tile_n, count // tile_m)
    stat_shape = jax.ShapeDtypeStruct((grid[0], count, 1), jnp.float32)
    stat_spec = pl.BlockSpec((1, tile_m, 1), lambda j, i: (j, i, 0))
    return pl.pallas_call(
        lambda *refs: stats_kernel(len(pieces), tile_n, *refs),
        grid=grid,
        in_specs=[
            pl.BlockSpec((tile_m, 1), lambda j, i: (i, 0)),
            pl.BlockSpec((tile_m, width_full), lambda j, i: (i, 0)),
        ]
        + [pl.BlockSpec((width, tile_n), lambda j, i: (0, j)) for _ in pieces],
        out_specs=[stat_spec, stat_spec, stat_spec],
        out_shape=[stat_shape, stat_shape, stat_shape],
        compiler_params=pltpu.CompilerParams(vmem_limit_bytes=48 * 1024 * 1024),
        cost_estimate=pl.CostEstimate(
            flops=2 * count * width_full * vocab,
            transcendentals=count * vocab,
            bytes_accessed=2 * width_full * vocab + 2 * count * width_full * grid[0],
        ),
    )(local_target.reshape(count, 1), rows, *pieces)


def body(
    token_ids,
    lengths,
    pack_dest,
    ref_hidden,
    reward_hidden,
    head_weight,
    norm_gain,
    score_weight,
    value_weight,
    old_logprob,
):
    shards = lax.axis_size("dp")
    ways = lax.axis_size("mp")
    me = lax.axis_index("dp")
    part = lax.axis_index("mp")
    req_dev, max_len, width_dev = ref_hidden.shape
    pair_len = max_len + 1
    slot_dev = shards * pair_len
    sub_len = slot_dev // ways
    blocks = sub_len // pair_len
    width_full = width_dev * ways
    steps = jnp.arange(max_len, dtype=jnp.int32)

    dest = lax.dynamic_slice_in_dim(pack_dest, me * req_dev, req_dev)
    size = lax.dynamic_slice_in_dim(lengths, me * req_dev, req_dev)
    rank = pair_rank(dest)
    row = dest[:, None] * pair_len + steps[None, :] + rank[:, None] * (pair_len - size[:, None])
    row = jnp.where(steps[None, :] < size[:, None], row, -1).reshape(-1)
    onehot = (row[None, :] == jnp.arange(slot_dev, dtype=jnp.int32)[:, None]).astype(jnp.bfloat16)
    ref_send = jnp.dot(
        onehot, ref_hidden.reshape(req_dev * max_len, width_dev), preferred_element_type=jnp.float32
    ).astype(jnp.bfloat16)
    reward_send = jnp.dot(
        onehot, reward_hidden.reshape(req_dev * max_len, width_dev), preferred_element_type=jnp.float32
    ).astype(jnp.bfloat16)
    reward_packed = lax.all_to_all(
        reward_send.reshape(shards, pair_len, width_dev), "dp", 0, 0, tiled=True
    ).reshape(slot_dev, width_dev)

    chips = ways // 2
    own_core = [head_weight] + [
        lax.ppermute(head_weight, "mp", [(i, (i + 2 * shift) % ways) for i in range(ways)])
        for shift in range(1, chips)
    ]
    mate_core = [lax.ppermute(block, "mp", [(i, i ^ 1) for i in range(ways)]) for block in own_core]
    chip, core = part // 2, part % 2
    order = jnp.arange(ways, dtype=jnp.int32)
    source_chip = (chip - order % chips) % chips
    source_core = jnp.where(order < chips, core, 1 - core)
    pick = (
        (source_chip * 2 + source_core)[:, None] == jnp.arange(ways, dtype=jnp.int32)[None, :]
    ).astype(jnp.bfloat16)

    parts_rows = lax.all_to_all(ref_send.reshape(ways, sub_len, width_dev), "mp", 0, 0, tiled=True)
    own_rows = jnp.einsum(
        "msf,nm->snf", parts_rows, pick, preferred_element_type=jnp.float32
    ).astype(jnp.bfloat16).reshape(sub_len, width_full)
    halves = 2
    half_len = sub_len // halves
    half_rows = [
        lax.all_gather(own_rows[h * half_len : (h + 1) * half_len], "dp", axis=0, tiled=True)
        for h in range(halves)
    ]

    dest_all = pack_dest.reshape(shards, req_dev)
    size_all = lengths.reshape(shards, req_dev)
    rank_all = pair_rank(dest_all)
    key = (
        dest_all[:, :, None] * pair_len
        + steps[None, None, :]
        + rank_all[:, :, None] * (pair_len - size_all[:, :, None])
        - part * sub_len
    )
    key = jnp.where(steps[None, None, :] < size_all[:, :, None], key, -1).reshape(shards, 1, -1)
    hits = key == jnp.arange(sub_len, dtype=jnp.int32)[None, :, None]
    targets = jnp.sum(
        jnp.where(hits, token_ids.reshape(shards, 1, -1), 0), axis=2
    ).reshape(-1)

    vocab_dev = head_weight.shape[1]
    local_target = (targets - me * vocab_dev).reshape(shards, halves, half_len)
    parts_stats = []
    for h in range(halves):
        tile_max, tile_total, tile_target = logit_stats(
            half_rows[h], own_core + mate_core, local_target[:, h].reshape(-1)
        )
        half_max = jnp.max(tile_max[:, :, 0], axis=0)
        half_total = jnp.sum(tile_total[:, :, 0] * jnp.exp(tile_max[:, :, 0] - half_max[None, :]), axis=0)
        half_target = jnp.sum(tile_target[:, :, 0], axis=0)
        parts_stats.append(jnp.stack([half_max, half_total, half_target]).reshape(3, shards, half_len))
    joint_stats = jnp.concatenate(parts_stats, axis=2)
    row_max, exp_total, target_logit = joint_stats[0], joint_stats[1], joint_stats[2]
    stats = jnp.stack([row_max, exp_total, target_logit]).reshape(3, shards, blocks, pair_len)
    to_shard = jnp.arange(shards, dtype=jnp.int32)[:, None] == (
        part * blocks + jnp.arange(blocks, dtype=jnp.int32)
    )[None, :]
    routed = jnp.sum(
        jnp.where(to_shard[:, None, None, :, None], stats[None], 0.0), axis=3
    )
    routed = lax.all_to_all(routed, "dp", 0, 0, tiled=True)
    joint_max = jnp.max(routed[:, 0], axis=0)
    joint_total = jnp.sum(routed[:, 1] * jnp.exp(routed[:, 0] - joint_max[None]), axis=0)
    joint_target = jnp.sum(routed[:, 2], axis=0)
    holder = me // blocks == part
    block_logprob = jnp.where(
        holder, joint_target - joint_max - jnp.log(joint_total), 0.0
    ).reshape(-1)

    hidden_f = reward_packed.astype(jnp.float32)
    sums = jnp.stack(
        [
            jnp.sum(hidden_f * hidden_f, axis=1),
            jnp.sum(hidden_f * (norm_gain * score_weight), axis=1),
            jnp.sum(hidden_f * (norm_gain * value_weight), axis=1),
        ]
    )
    ref_logprob, squares, score_dot, value_dot = lax.psum(
        jnp.concatenate([block_logprob[None], sums]), "mp"
    )
    inv_rms = lax.rsqrt(squares / width_full + norm_eps)
    score = score_dot * inv_rms
    value_est = value_dot * inv_rms

    mine = (pack_dest.reshape(shards, req_dev) == me).astype(jnp.int32)
    is_first = jnp.logical_and(mine == 1, jnp.cumsum(mine, axis=1) == 1)
    first_len = jnp.sum(jnp.where(is_first, lengths.reshape(shards, req_dev), 0), axis=1)
    place = jnp.arange(pair_len, dtype=jnp.int32)[None, :]
    is_last = jnp.logical_or(place == first_len[:, None] - 1, place == pair_len - 1)
    is_last_flat = is_last.reshape(-1)

    reward = -kl_coef * (old_logprob - ref_logprob) + jnp.where(is_last_flat, score, 0.0)
    next_value = jnp.concatenate([value_est[1:], jnp.zeros((1,), jnp.float32)])
    not_last = 1.0 - is_last_flat.astype(jnp.float32)
    td_error = (reward + discount * next_value * not_last - value_est).reshape(shards, pair_len)
    decay = discount * gae_mix
    carry = td_error[:, pair_len - 1]
    columns = [carry]
    for step in range(pair_len - 2, -1, -1):
        carry = td_error[:, step] + decay * jnp.where(is_last[:, step], 0.0, carry)
        columns.append(carry)
    advantage = jnp.stack(columns[::-1], axis=1).reshape(-1)
    return (ref_logprob, advantage)


def solution(mesh):
    return jax.shard_map(
        body,
        mesh=mesh,
        in_specs=(
            P(),
            P(),
            P(),
            P("dp", None, "mp"),
            P("dp", None, "mp"),
            P("mp", "dp"),
            P("mp"),
            P("mp"),
            P("mp"),
            P("dp"),
        ),
        out_specs=(P("dp"), P("dp")),
        check_vma=False,
    )
```

```python
import jax
import jax.numpy as jnp
from jax import lax
from jax.experimental import pallas as pl
from jax.experimental.pallas import tpu as pltpu
from jax.sharding import PartitionSpec as P


kl_coef = 0.1
discount = 0.99
gae_mix = 0.95
norm_eps = 1e-05


def pair_rank(dest):
    count = dest.shape[-1]
    idx = jnp.arange(count, dtype=jnp.int32)
    same = dest[..., None, :] == dest[..., :, None]
    earlier = idx[None, :] < idx[:, None]
    return jnp.sum(jnp.logical_and(same, earlier).astype(jnp.int32), axis=-1)


def stats_kernel(pieces, tile_n, target_ref, rows_ref, *refs):
    weight_refs = refs[:pieces]
    max_ref, total_ref, target_logit_ref = refs[pieces:]
    width = weight_refs[0].shape[0]
    logits = jnp.dot(rows_ref[:, 0:width], weight_refs[0][...], preferred_element_type=jnp.float32)
    for k in range(1, pieces):
        logits = logits + jnp.dot(
            rows_ref[:, k * width : (k + 1) * width],
            weight_refs[k][...],
            preferred_element_type=jnp.float32,
        )
    row_max = jnp.max(logits, axis=1, keepdims=True)
    total = jnp.sum(jnp.exp(logits - row_max), axis=1, keepdims=True)
    column = lax.broadcasted_iota(jnp.int32, logits.shape, 1) + pl.program_id(0) * tile_n
    target_logit = jnp.sum(jnp.where(column == target_ref[...], logits, 0.0), axis=1, keepdims=True)
    max_ref[0] = row_max
    total_ref[0] = total
    target_logit_ref[0] = target_logit


def logit_stats(rows, pieces, local_target, tile_m=256, tile_n=1024):
    count, width_full = rows.shape
    width, vocab = pieces[0].shape
    grid = (vocab // tile_n, count // tile_m)
    stat_shape = jax.ShapeDtypeStruct((grid[0], count, 1), jnp.float32)
    stat_spec = pl.BlockSpec((1, tile_m, 1), lambda j, i: (j, i, 0))
    return pl.pallas_call(
        lambda *refs: stats_kernel(len(pieces), tile_n, *refs),
        grid=grid,
        in_specs=[
            pl.BlockSpec((tile_m, 1), lambda j, i: (i, 0)),
            pl.BlockSpec((tile_m, width_full), lambda j, i: (i, 0)),
        ]
        + [pl.BlockSpec((width, tile_n), lambda j, i: (0, j)) for _ in pieces],
        out_specs=[stat_spec, stat_spec, stat_spec],
        out_shape=[stat_shape, stat_shape, stat_shape],
        compiler_params=pltpu.CompilerParams(vmem_limit_bytes=48 * 1024 * 1024),
        cost_estimate=pl.CostEstimate(
            flops=2 * count * width_full * vocab,
            transcendentals=count * vocab,
            bytes_accessed=2 * width_full * vocab + 2 * count * width_full * grid[0],
        ),
    )(local_target.reshape(count, 1), rows, *pieces)


def body(
    token_ids,
    lengths,
    pack_dest,
    ref_hidden,
    reward_hidden,
    head_weight,
    norm_gain,
    score_weight,
    value_weight,
    old_logprob,
):
    shards = lax.axis_size("dp")
    ways = lax.axis_size("mp")
    me = lax.axis_index("dp")
    part = lax.axis_index("mp")
    req_dev, max_len, width_dev = ref_hidden.shape
    pair_len = max_len + 1
    slot_dev = shards * pair_len
    sub_len = slot_dev // ways
    blocks = sub_len // pair_len
    width_full = width_dev * ways
    steps = jnp.arange(max_len, dtype=jnp.int32)

    dest = lax.dynamic_slice_in_dim(pack_dest, me * req_dev, req_dev)
    size = lax.dynamic_slice_in_dim(lengths, me * req_dev, req_dev)
    rank = pair_rank(dest)
    row = dest[:, None] * pair_len + steps[None, :] + rank[:, None] * (pair_len - size[:, None])
    row = jnp.where(steps[None, :] < size[:, None], row, -1).reshape(-1)
    onehot = (row[None, :] == jnp.arange(slot_dev, dtype=jnp.int32)[:, None]).astype(jnp.bfloat16)
    ref_send = jnp.dot(
        onehot, ref_hidden.reshape(req_dev * max_len, width_dev), preferred_element_type=jnp.float32
    ).astype(jnp.bfloat16)
    reward_send = jnp.dot(
        onehot, reward_hidden.reshape(req_dev * max_len, width_dev), preferred_element_type=jnp.float32
    ).astype(jnp.bfloat16)
    reward_packed = lax.all_to_all(
        reward_send.reshape(shards, pair_len, width_dev), "dp", 0, 0, tiled=True
    ).reshape(slot_dev, width_dev)

    chips = ways // 2
    own_core = [head_weight] + [
        lax.ppermute(head_weight, "mp", [(i, (i + 2 * shift) % ways) for i in range(ways)])
        for shift in range(1, chips)
    ]
    mate_core = [lax.ppermute(block, "mp", [(i, i ^ 1) for i in range(ways)]) for block in own_core]
    chip, core = part // 2, part % 2
    order = jnp.arange(ways, dtype=jnp.int32)
    source_chip = (chip - order % chips) % chips
    source_core = jnp.where(order < chips, core, 1 - core)
    pick = (
        (source_chip * 2 + source_core)[:, None] == jnp.arange(ways, dtype=jnp.int32)[None, :]
    ).astype(jnp.bfloat16)

    parts_rows = lax.all_to_all(ref_send.reshape(ways, sub_len, width_dev), "mp", 0, 0, tiled=True)
    own_rows = jnp.einsum(
        "msf,nm->snf", parts_rows, pick, preferred_element_type=jnp.float32
    ).astype(jnp.bfloat16).reshape(sub_len, width_full)
    block_rows = lax.all_gather(own_rows, "dp", axis=0, tiled=True)

    dest_all = pack_dest.reshape(shards, req_dev)
    size_all = lengths.reshape(shards, req_dev)
    rank_all = pair_rank(dest_all)
    key = (
        dest_all[:, :, None] * pair_len
        + steps[None, None, :]
        + rank_all[:, :, None] * (pair_len - size_all[:, :, None])
        - part * sub_len
    )
    key = jnp.where(steps[None, None, :] < size_all[:, :, None], key, -1).reshape(shards, 1, -1)
    hits = key == jnp.arange(sub_len, dtype=jnp.int32)[None, :, None]
    targets = jnp.sum(
        jnp.where(hits, token_ids.reshape(shards, 1, -1), 0), axis=2
    ).reshape(-1)

    vocab_dev = head_weight.shape[1]
    tile_max, tile_total, tile_target = logit_stats(
        block_rows, own_core + mate_core, targets - me * vocab_dev
    )
    row_max = jnp.max(tile_max[:, :, 0], axis=0)
    exp_total = jnp.sum(tile_total[:, :, 0] * jnp.exp(tile_max[:, :, 0] - row_max[None, :]), axis=0)
    target_logit = jnp.sum(tile_target[:, :, 0], axis=0)
    stats = jnp.stack([row_max, exp_total, target_logit]).reshape(3, shards, blocks, pair_len)
    to_shard = jnp.arange(shards, dtype=jnp.int32)[:, None] == (
        part * blocks + jnp.arange(blocks, dtype=jnp.int32)
    )[None, :]
    routed = jnp.sum(
        jnp.where(to_shard[:, None, None, :, None], stats[None], 0.0), axis=3
    )
    routed = lax.all_to_all(routed, "dp", 0, 0, tiled=True)
    joint_max = jnp.max(routed[:, 0], axis=0)
    joint_total = jnp.sum(routed[:, 1] * jnp.exp(routed[:, 0] - joint_max[None]), axis=0)
    joint_target = jnp.sum(routed[:, 2], axis=0)
    holder = me // blocks == part
    block_logprob = jnp.where(
        holder, joint_target - joint_max - jnp.log(joint_total), 0.0
    ).reshape(-1)

    hidden_f = reward_packed.astype(jnp.float32)
    sums = jnp.stack(
        [
            jnp.sum(hidden_f * hidden_f, axis=1),
            jnp.sum(hidden_f * (norm_gain * score_weight), axis=1),
            jnp.sum(hidden_f * (norm_gain * value_weight), axis=1),
        ]
    )
    squares, score_dot, value_dot = lax.psum(sums, "mp")
    ref_logprob = block_logprob
    for shift in range(1, ways):
        ref_logprob = ref_logprob + lax.ppermute(
            block_logprob, "mp", [(i, (i + shift) % ways) for i in range(ways)]
        )
    inv_rms = lax.rsqrt(squares / width_full + norm_eps)
    score = score_dot * inv_rms
    value_est = value_dot * inv_rms

    mine = (pack_dest.reshape(shards, req_dev) == me).astype(jnp.int32)
    is_first = jnp.logical_and(mine == 1, jnp.cumsum(mine, axis=1) == 1)
    first_len = jnp.sum(jnp.where(is_first, lengths.reshape(shards, req_dev), 0), axis=1)
    place = jnp.arange(pair_len, dtype=jnp.int32)[None, :]
    is_last = jnp.logical_or(place == first_len[:, None] - 1, place == pair_len - 1)
    is_last_flat = is_last.reshape(-1)

    reward = -kl_coef * (old_logprob - ref_logprob) + jnp.where(is_last_flat, score, 0.0)
    next_value = jnp.concatenate([value_est[1:], jnp.zeros((1,), jnp.float32)])
    not_last = 1.0 - is_last_flat.astype(jnp.float32)
    td_error = (reward + discount * next_value * not_last - value_est).reshape(shards, pair_len)
    decay = discount * gae_mix
    carry = td_error[:, pair_len - 1]
    columns = [carry]
    for step in range(pair_len - 2, -1, -1):
        carry = td_error[:, step] + decay * jnp.where(is_last[:, step], 0.0, carry)
        columns.append(carry)
    advantage = jnp.stack(columns[::-1], axis=1).reshape(-1)
    return (ref_logprob, advantage)


def solution(mesh):
    return jax.shard_map(
        body,
        mesh=mesh,
        in_specs=(
            P(),
            P(),
            P(),
            P("dp", None, "mp"),
            P("dp", None, "mp"),
            P("mp", "dp"),
            P("mp"),
            P("mp"),
            P("mp"),
            P("dp"),
        ),
        out_specs=(P("dp"), P("dp")),
        check_vma=False,
    )
```

```python
import functools

import jax
import numpy as np
import jax.numpy as jnp
from jax import lax
from jax.experimental import pallas as pl
from jax.experimental.pallas import tpu as pltpu
from jax.sharding import PartitionSpec as P

kl_coef = 0.1
discount = 0.99
gae_mix = 0.95
norm_eps = 1e-05


def pair_rank(dest):
    count = dest.shape[-1]
    idx = jnp.arange(count, dtype=jnp.int32)
    same = dest[..., None, :] == dest[..., :, None]
    earlier = idx[None, :] < idx[:, None]
    return jnp.sum(jnp.logical_and(same, earlier).astype(jnp.int32), axis=-1)


def stats_kernel(heights, tile_n, target_ref, rows_ref, *refs):
    pieces = len(heights)
    weight_refs = refs[:pieces]
    max_ref, total_ref, target_logit_ref = refs[pieces:]
    logits = None
    offset = 0
    for k, height in enumerate(heights):
        part = jnp.dot(
            rows_ref[:, offset : offset + height], weight_refs[k][...], preferred_element_type=jnp.float32
        )
        logits = part if logits is None else logits + part
        offset += height
    row_max = jnp.max(logits, axis=1, keepdims=True)
    total = jnp.sum(jnp.exp(logits - row_max), axis=1, keepdims=True)
    column = lax.broadcasted_iota(jnp.int32, logits.shape, 1) + pl.program_id(0) * tile_n
    target_logit = jnp.sum(jnp.where(column == target_ref[...], logits, 0.0), axis=1, keepdims=True)
    max_ref[0] = row_max
    total_ref[0] = total
    target_logit_ref[0] = target_logit


def logit_stats(rows, pieces, local_target, tile_m=256, tile_n=1024):
    count, width_full = rows.shape
    vocab = pieces[0].shape[1]
    heights = tuple(piece.shape[0] for piece in pieces)
    grid = (vocab // tile_n, count // tile_m)
    stat_shape = jax.ShapeDtypeStruct((grid[0], count, 1), jnp.float32)
    stat_spec = pl.BlockSpec((1, tile_m, 1), lambda j, i: (j, i, 0))
    return pl.pallas_call(
        lambda *refs: stats_kernel(heights, tile_n, *refs),
        grid=grid,
        in_specs=[
            pl.BlockSpec((tile_m, 1), lambda j, i: (i, 0)),
            pl.BlockSpec((tile_m, width_full), lambda j, i: (i, 0)),
        ]
        + [pl.BlockSpec((height, tile_n), lambda j, i: (0, j)) for height in heights],
        out_specs=[stat_spec, stat_spec, stat_spec],
        out_shape=[stat_shape, stat_shape, stat_shape],
        compiler_params=pltpu.CompilerParams(vmem_limit_bytes=48 * 1024 * 1024),
        cost_estimate=pl.CostEstimate(
            flops=2 * count * width_full * vocab,
            transcendentals=count * vocab,
            bytes_accessed=2 * width_full * vocab + 2 * count * width_full * grid[0],
        ),
    )(local_target.reshape(count, 1), rows, *pieces)


def ring_perm(places, step):
    zs, xs = places.shape
    where = {int(places[z, x]): (z, x) for z in range(zs) for x in range(xs)}
    return [
        (i, int(places[(z + step[0]) % zs, (x + step[1]) % xs])) for i, (z, x) in sorted(where.items())
    ]


def body(
    places,
    token_ids,
    lengths,
    pack_dest,
    ref_hidden,
    reward_hidden,
    head_weight,
    norm_gain,
    score_weight,
    value_weight,
    old_logprob,
):
    shards = lax.axis_size("dp")
    ways = lax.axis_size("mp")
    me = lax.axis_index("dp")
    part = lax.axis_index("mp")
    req_dev, max_len, width_dev = ref_hidden.shape
    pair_len = max_len + 1
    slot_dev = shards * pair_len
    sub_len = slot_dev // ways
    blocks = sub_len // pair_len
    width_full = width_dev * ways
    steps = jnp.arange(max_len, dtype=jnp.int32)

    dest = lax.dynamic_slice_in_dim(pack_dest, me * req_dev, req_dev)
    size = lax.dynamic_slice_in_dim(lengths, me * req_dev, req_dev)
    rank = pair_rank(dest)
    row = dest[:, None] * pair_len + steps[None, :] + rank[:, None] * (pair_len - size[:, None])
    row = jnp.where(steps[None, :] < size[:, None], row, -1).reshape(-1)
    onehot = (row[None, :] == jnp.arange(slot_dev, dtype=jnp.int32)[:, None]).astype(jnp.bfloat16)
    ref_send = jnp.dot(
        onehot, ref_hidden.reshape(req_dev * max_len, width_dev), preferred_element_type=jnp.float32
    ).astype(jnp.bfloat16)
    reward_send = jnp.dot(
        onehot, reward_hidden.reshape(req_dev * max_len, width_dev), preferred_element_type=jnp.float32
    ).astype(jnp.bfloat16)
    reward_packed = lax.all_to_all(
        reward_send.reshape(shards, pair_len, width_dev), "dp", 0, 0, tiled=True
    ).reshape(slot_dev, width_dev)

    chips = ways // 2
    half = width_dev // 2

    def along_y(x, shift):
        return lax.ppermute(x, "mp", [(i, ((i // 2 + shift) % chips) * 2 + i % 2) for i in range(ways)])

    from_prev = along_y(head_weight, 1)
    from_next = along_y(head_weight, -1)
    own_core = [
        head_weight,
        from_prev,
        from_next,
        along_y(from_prev[:half], 1),
        along_y(from_next[half:], -1),
    ]
    mate_core = [lax.ppermute(block, "mp", [(i, i ^ 1) for i in range(ways)]) for block in own_core]
    chip, core = part // 2, part % 2
    order = jnp.arange(ways, dtype=jnp.int32)
    chip_step = jnp.array([0, -1, 1, -2], jnp.int32)
    source_chip = (chip + chip_step[order % chips]) % chips
    source_core = jnp.where(order < chips, core, 1 - core)
    pick = (
        (source_chip * 2 + source_core)[:, None] == jnp.arange(ways, dtype=jnp.int32)[None, :]
    ).astype(jnp.bfloat16)

    parts_rows = lax.all_to_all(ref_send.reshape(ways, sub_len, width_dev), "mp", 0, 0, tiled=True)
    own_rows = jnp.einsum(
        "msf,nm->snf", parts_rows, pick, preferred_element_type=jnp.float32
    ).astype(jnp.bfloat16).reshape(sub_len, width_full)

    zs, xs = places.shape
    x_fwd = lax.ppermute(own_rows, "dp", ring_perm(places, (0, 1)))
    x_back = lax.ppermute(own_rows, "dp", ring_perm(places, (0, -1)))
    x_far = lax.ppermute(x_fwd, "dp", ring_perm(places, (0, 1)))
    x_steps = [0, -1, 1, -2]
    group = jnp.stack([own_rows, x_fwd, x_back, x_far])
    z_groups = [group]
    z_steps = [0]
    fwd, back = group, group
    for hop in range(1, zs // 2):
        fwd = lax.ppermute(fwd, "dp", ring_perm(places, (1, 0)))
        back = lax.ppermute(back, "dp", ring_perm(places, (-1, 0)))
        z_groups += [fwd, back]
        z_steps += [-hop, hop]
    split = len(x_steps) // 2
    far_a = lax.ppermute(fwd[:split], "dp", ring_perm(places, (1, 0)))
    far_b = lax.ppermute(back[split:], "dp", ring_perm(places, (-1, 0)))
    z_groups.append(jnp.concatenate([far_a, far_b]))
    z_steps.append(-(zs // 2))
    block_rows = jnp.concatenate(z_groups).reshape(-1, width_full)
    my_z = jnp.argmax(jnp.any(places == me, axis=1))
    my_x = jnp.argmax(jnp.any(places == me, axis=0))
    places_arr = jnp.asarray(places, jnp.int32)
    source_shard = jnp.stack(
        [places_arr[(my_z + dz) % zs, (my_x + dx) % xs] for dz in z_steps for dx in x_steps]
    )
    is_source = source_shard[:, None] == jnp.arange(shards, dtype=jnp.int32)[None, :]

    dest_all = pack_dest.reshape(shards, req_dev)
    size_all = lengths.reshape(shards, req_dev)
    rank_all = pair_rank(dest_all)
    key = (
        dest_all[:, :, None] * pair_len
        + steps[None, None, :]
        + rank_all[:, :, None] * (pair_len - size_all[:, :, None])
        - part * sub_len
    )
    key = jnp.where(steps[None, None, :] < size_all[:, :, None], key, -1).reshape(shards, 1, -1)
    hits = key == jnp.arange(sub_len, dtype=jnp.int32)[None, :, None]
    targets = jnp.sum(jnp.where(hits, token_ids.reshape(shards, 1, -1), 0), axis=2)
    targets = jnp.sum(jnp.where(is_source[:, :, None], targets[None], 0), axis=1).reshape(-1)

    vocab_dev = head_weight.shape[1]
    tile_max, tile_total, tile_target = logit_stats(
        block_rows, own_core + mate_core, targets - me * vocab_dev
    )
    row_max = jnp.max(tile_max[:, :, 0], axis=0)
    exp_total = jnp.sum(tile_total[:, :, 0] * jnp.exp(tile_max[:, :, 0] - row_max[None, :]), axis=0)
    target_logit = jnp.sum(tile_target[:, :, 0], axis=0)
    stats = jnp.stack([row_max, exp_total, target_logit]).reshape(3, shards, 1, sub_len)
    stats = jnp.sum(jnp.where(is_source[None, :, :, None], stats, 0.0), axis=1)
    stats = stats.reshape(3, shards, blocks, pair_len)
    to_shard = jnp.arange(shards, dtype=jnp.int32)[:, None] == (
        part * blocks + jnp.arange(blocks, dtype=jnp.int32)
    )[None, :]
    routed = jnp.sum(
        jnp.where(to_shard[:, None, None, :, None], stats[None], 0.0), axis=3
    )
    routed = lax.all_to_all(routed, "dp", 0, 0, tiled=True)
    joint_max = jnp.max(routed[:, 0], axis=0)
    joint_total = jnp.sum(routed[:, 1] * jnp.exp(routed[:, 0] - joint_max[None]), axis=0)
    joint_target = jnp.sum(routed[:, 2], axis=0)
    holder = me // blocks == part
    block_logprob = jnp.where(
        holder, joint_target - joint_max - jnp.log(joint_total), 0.0
    ).reshape(-1)

    hidden_f = reward_packed.astype(jnp.float32)
    sums = jnp.stack(
        [
            jnp.sum(hidden_f * hidden_f, axis=1),
            jnp.sum(hidden_f * (norm_gain * score_weight), axis=1),
            jnp.sum(hidden_f * (norm_gain * value_weight), axis=1),
        ]
    )
    ref_logprob, squares, score_dot, value_dot = lax.psum(
        jnp.concatenate([block_logprob[None], sums]), "mp"
    )
    inv_rms = lax.rsqrt(squares / width_full + norm_eps)
    score = score_dot * inv_rms
    value_est = value_dot * inv_rms

    mine = (pack_dest.reshape(shards, req_dev) == me).astype(jnp.int32)
    is_first = jnp.logical_and(mine == 1, jnp.cumsum(mine, axis=1) == 1)
    first_len = jnp.sum(jnp.where(is_first, lengths.reshape(shards, req_dev), 0), axis=1)
    place = jnp.arange(pair_len, dtype=jnp.int32)[None, :]
    is_last = jnp.logical_or(place == first_len[:, None] - 1, place == pair_len - 1)
    is_last_flat = is_last.reshape(-1)

    reward = -kl_coef * (old_logprob - ref_logprob) + jnp.where(is_last_flat, score, 0.0)
    next_value = jnp.concatenate([value_est[1:], jnp.zeros((1,), jnp.float32)])
    not_last = 1.0 - is_last_flat.astype(jnp.float32)
    td_error = (reward + discount * next_value * not_last - value_est).reshape(shards, pair_len)
    decay = discount * gae_mix
    carry = td_error[:, pair_len - 1]
    columns = [carry]
    for step in range(pair_len - 2, -1, -1):
        carry = td_error[:, step] + decay * jnp.where(is_last[:, step], 0.0, carry)
        columns.append(carry)
    advantage = jnp.stack(columns[::-1], axis=1).reshape(-1)
    return (ref_logprob, advantage)


def solution(mesh):
    dp_devices = mesh.devices[:, 0]
    zs = sorted({d.coords[2] for d in dp_devices})
    xs = sorted({d.coords[0] for d in dp_devices})
    places = np.zeros((len(zs), len(xs)), np.int32)
    for i, d in enumerate(dp_devices):
        places[zs.index(d.coords[2]), xs.index(d.coords[0])] = i
    return jax.shard_map(
        functools.partial(body, places),
        mesh=mesh,
        in_specs=(
            P(),
            P(),
            P(),
            P("dp", None, "mp"),
            P("dp", None, "mp"),
            P("mp", "dp"),
            P("mp"),
            P("mp"),
            P("mp"),
            P("dp"),
        ),
        out_specs=(P("dp"), P("dp")),
        check_vma=False,
    )
```

```python
import functools

import jax
import numpy as np
import jax.numpy as jnp
from jax import lax
from jax.experimental import pallas as pl
from jax.experimental.pallas import tpu as pltpu
from jax.sharding import PartitionSpec as P

kl_coef = 0.1
discount = 0.99
gae_mix = 0.95
norm_eps = 1e-05


def pair_rank(dest):
    count = dest.shape[-1]
    idx = jnp.arange(count, dtype=jnp.int32)
    same = dest[..., None, :] == dest[..., :, None]
    earlier = idx[None, :] < idx[:, None]
    return jnp.sum(jnp.logical_and(same, earlier).astype(jnp.int32), axis=-1)


def stats_kernel(heights, tile_n, target_ref, rows_ref, *refs):
    pieces = len(heights)
    weight_refs = refs[:pieces]
    max_ref, total_ref, target_logit_ref = refs[pieces:]
    logits = None
    offset = 0
    for k, height in enumerate(heights):
        part = jnp.dot(
            rows_ref[:, offset : offset + height], weight_refs[k][...], preferred_element_type=jnp.float32
        )
        logits = part if logits is None else logits + part
        offset += height
    row_max = jnp.max(logits, axis=1, keepdims=True)
    total = jnp.sum(jnp.exp(logits - row_max), axis=1, keepdims=True)
    column = lax.broadcasted_iota(jnp.int32, logits.shape, 1) + pl.program_id(0) * tile_n
    target_logit = jnp.sum(jnp.where(column == target_ref[...], logits, 0.0), axis=1, keepdims=True)
    max_ref[0] = row_max
    total_ref[0] = total
    target_logit_ref[0] = target_logit


def logit_stats(rows, pieces, local_target, tile_m=256, tile_n=1024):
    count, width_full = rows.shape
    vocab = pieces[0].shape[1]
    heights = tuple(piece.shape[0] for piece in pieces)
    grid = (vocab // tile_n, count // tile_m)
    stat_shape = jax.ShapeDtypeStruct((grid[0], count, 1), jnp.float32)
    stat_spec = pl.BlockSpec((1, tile_m, 1), lambda j, i: (j, i, 0))
    return pl.pallas_call(
        lambda *refs: stats_kernel(heights, tile_n, *refs),
        grid=grid,
        in_specs=[
            pl.BlockSpec((tile_m, 1), lambda j, i: (i, 0)),
            pl.BlockSpec((tile_m, width_full), lambda j, i: (i, 0)),
        ]
        + [pl.BlockSpec((height, tile_n), lambda j, i: (0, j)) for height in heights],
        out_specs=[stat_spec, stat_spec, stat_spec],
        out_shape=[stat_shape, stat_shape, stat_shape],
        compiler_params=pltpu.CompilerParams(vmem_limit_bytes=48 * 1024 * 1024),
        cost_estimate=pl.CostEstimate(
            flops=2 * count * width_full * vocab,
            transcendentals=count * vocab,
            bytes_accessed=2 * width_full * vocab + 2 * count * width_full * grid[0],
        ),
    )(local_target.reshape(count, 1), rows, *pieces)


def ring_perm(places, step):
    zs, xs = places.shape
    where = {int(places[z, x]): (z, x) for z in range(zs) for x in range(xs)}
    return [
        (i, int(places[(z + step[0]) % zs, (x + step[1]) % xs])) for i, (z, x) in sorted(where.items())
    ]


def ring_offsets(size):
    offsets = [0]
    for hop in range(1, (size + 1) // 2):
        offsets += [-hop, hop]
    if size % 2 == 0:
        offsets.append(-(size // 2))
    return offsets


def ring_axis(group, places, axis):
    size = places.shape[axis]
    step = [0, 0]
    step[axis] = 1
    ahead, behind = tuple(step), tuple(-v for v in step)
    blocks = [group]
    fwd, back = group, group
    for hop in range(1, (size + 1) // 2):
        fwd = lax.ppermute(fwd, "dp", ring_perm(places, ahead))
        back = lax.ppermute(back, "dp", ring_perm(places, behind))
        blocks += [fwd, back]
    if size % 2 == 0:
        dim = 0 if group.shape[0] > 1 else 1
        cut = group.shape[dim] // 2
        far_a = lax.ppermute(lax.slice_in_dim(fwd, 0, cut, axis=dim), "dp", ring_perm(places, ahead))
        far_b = lax.ppermute(
            lax.slice_in_dim(back, cut, group.shape[dim], axis=dim), "dp", ring_perm(places, behind)
        )
        blocks.append(jnp.concatenate([far_a, far_b], axis=dim))
    return jnp.concatenate(blocks)


def source_tables(places):
    zs, xs = places.shape
    first, second = [], []
    for i in range(zs * xs):
        z, x = [int(v[0]) for v in np.nonzero(places == i)]
        first.append(
            [places[(z + dz) % zs, (x + dx) % xs] for dx in ring_offsets(xs) for dz in ring_offsets(zs)]
        )
        second.append(
            [places[(z + dz) % zs, (x + dx) % xs] for dz in ring_offsets(zs) for dx in ring_offsets(xs)]
        )
    return np.array(first, np.int32), np.array(second, np.int32)


def body(
    places,
    tables,
    token_ids,
    lengths,
    pack_dest,
    ref_hidden,
    reward_hidden,
    head_weight,
    norm_gain,
    score_weight,
    value_weight,
    old_logprob,
):
    shards = lax.axis_size("dp")
    ways = lax.axis_size("mp")
    me = lax.axis_index("dp")
    part = lax.axis_index("mp")
    req_dev, max_len, width_dev = ref_hidden.shape
    pair_len = max_len + 1
    slot_dev = shards * pair_len
    sub_len = slot_dev // ways
    blocks = sub_len // pair_len
    width_full = width_dev * ways
    steps = jnp.arange(max_len, dtype=jnp.int32)

    dest = lax.dynamic_slice_in_dim(pack_dest, me * req_dev, req_dev)
    size = lax.dynamic_slice_in_dim(lengths, me * req_dev, req_dev)
    rank = pair_rank(dest)
    row = dest[:, None] * pair_len + steps[None, :] + rank[:, None] * (pair_len - size[:, None])
    row = jnp.where(steps[None, :] < size[:, None], row, -1).reshape(-1)
    onehot = (row[None, :] == jnp.arange(slot_dev, dtype=jnp.int32)[:, None]).astype(jnp.bfloat16)
    ref_send = jnp.dot(
        onehot, ref_hidden.reshape(req_dev * max_len, width_dev), preferred_element_type=jnp.float32
    ).astype(jnp.bfloat16)
    reward_send = jnp.dot(
        onehot, reward_hidden.reshape(req_dev * max_len, width_dev), preferred_element_type=jnp.float32
    ).astype(jnp.bfloat16)
    reward_packed = lax.all_to_all(
        reward_send.reshape(shards, pair_len, width_dev), "dp", 0, 0, tiled=True
    ).reshape(slot_dev, width_dev)

    chips = ways // 2
    half = width_dev // 2

    def along_y(x, shift):
        return lax.ppermute(x, "mp", [(i, ((i // 2 + shift) % chips) * 2 + i % 2) for i in range(ways)])

    from_prev = along_y(head_weight, 1)
    from_next = along_y(head_weight, -1)
    own_core = [
        head_weight,
        from_prev,
        from_next,
        along_y(from_prev[:half], 1),
        along_y(from_next[half:], -1),
    ]
    mate_core = [lax.ppermute(block, "mp", [(i, i ^ 1) for i in range(ways)]) for block in own_core]
    chip, core = part // 2, part % 2
    order = jnp.arange(ways, dtype=jnp.int32)
    chip_step = jnp.array([0, -1, 1, -2], jnp.int32)
    source_chip = (chip + chip_step[order % chips]) % chips
    source_core = jnp.where(order < chips, core, 1 - core)
    pick = (
        (source_chip * 2 + source_core)[:, None] == jnp.arange(ways, dtype=jnp.int32)[None, :]
    ).astype(jnp.bfloat16)

    parts_rows = lax.all_to_all(ref_send.reshape(ways, sub_len, width_dev), "mp", 0, 0, tiled=True)
    own_rows = jnp.einsum(
        "msf,nm->snf", parts_rows, pick, preferred_element_type=jnp.float32
    ).astype(jnp.bfloat16).reshape(sub_len, width_full)

    half_len = sub_len // 2
    first = ring_axis(ring_axis(own_rows[None, :half_len], places, 0), places, 1)
    second = ring_axis(ring_axis(own_rows[None, half_len:], places, 1), places, 0)
    block_rows = jnp.concatenate([first, second]).reshape(-1, width_full)
    source_first = jnp.asarray(tables[0])[me]
    source_second = jnp.asarray(tables[1])[me]
    shard_ids = jnp.arange(shards, dtype=jnp.int32)[None, :]
    is_source = [source_first[:, None] == shard_ids, source_second[:, None] == shard_ids]

    dest_all = pack_dest.reshape(shards, req_dev)
    size_all = lengths.reshape(shards, req_dev)
    rank_all = pair_rank(dest_all)
    key = (
        dest_all[:, :, None] * pair_len
        + steps[None, None, :]
        + rank_all[:, :, None] * (pair_len - size_all[:, :, None])
        - part * sub_len
    )
    key = jnp.where(steps[None, None, :] < size_all[:, :, None], key, -1).reshape(shards, 1, -1)
    hits = key == jnp.arange(sub_len, dtype=jnp.int32)[None, :, None]
    targets = jnp.sum(jnp.where(hits, token_ids.reshape(shards, 1, -1), 0), axis=2)
    targets = targets.reshape(shards, 2, half_len)
    targets = jnp.concatenate(
        [
            jnp.sum(jnp.where(is_source[h][:, :, None], targets[None, :, h], 0), axis=1)
            for h in range(2)
        ]
    ).reshape(-1)

    vocab_dev = head_weight.shape[1]
    tile_max, tile_total, tile_target = logit_stats(
        block_rows, own_core + mate_core, targets - me * vocab_dev
    )
    row_max = jnp.max(tile_max[:, :, 0], axis=0)
    exp_total = jnp.sum(tile_total[:, :, 0] * jnp.exp(tile_max[:, :, 0] - row_max[None, :]), axis=0)
    target_logit = jnp.sum(tile_target[:, :, 0], axis=0)
    stats = jnp.stack([row_max, exp_total, target_logit]).reshape(3, 2, shards, 1, half_len)
    stats = jnp.stack(
        [jnp.sum(jnp.where(is_source[h][None, :, :, None], stats[:, h], 0.0), axis=1) for h in range(2)],
        axis=2,
    )
    stats = stats.reshape(3, shards, blocks, pair_len)
    to_shard = jnp.arange(shards, dtype=jnp.int32)[:, None] == (
        part * blocks + jnp.arange(blocks, dtype=jnp.int32)
    )[None, :]
    routed = jnp.sum(
        jnp.where(to_shard[:, None, None, :, None], stats[None], 0.0), axis=3
    )
    routed = lax.all_to_all(routed, "dp", 0, 0, tiled=True)
    joint_max = jnp.max(routed[:, 0], axis=0)
    joint_total = jnp.sum(routed[:, 1] * jnp.exp(routed[:, 0] - joint_max[None]), axis=0)
    joint_target = jnp.sum(routed[:, 2], axis=0)
    holder = me // blocks == part
    block_logprob = jnp.where(
        holder, joint_target - joint_max - jnp.log(joint_total), 0.0
    ).reshape(-1)

    hidden_f = reward_packed.astype(jnp.float32)
    sums = jnp.stack(
        [
            jnp.sum(hidden_f * hidden_f, axis=1),
            jnp.sum(hidden_f * (norm_gain * score_weight), axis=1),
            jnp.sum(hidden_f * (norm_gain * value_weight), axis=1),
        ]
    )
    ref_logprob, squares, score_dot, value_dot = lax.psum(
        jnp.concatenate([block_logprob[None], sums]), "mp"
    )
    inv_rms = lax.rsqrt(squares / width_full + norm_eps)
    score = score_dot * inv_rms
    value_est = value_dot * inv_rms

    mine = (pack_dest.reshape(shards, req_dev) == me).astype(jnp.int32)
    is_first = jnp.logical_and(mine == 1, jnp.cumsum(mine, axis=1) == 1)
    first_len = jnp.sum(jnp.where(is_first, lengths.reshape(shards, req_dev), 0), axis=1)
    place = jnp.arange(pair_len, dtype=jnp.int32)[None, :]
    is_last = jnp.logical_or(place == first_len[:, None] - 1, place == pair_len - 1)
    is_last_flat = is_last.reshape(-1)

    reward = -kl_coef * (old_logprob - ref_logprob) + jnp.where(is_last_flat, score, 0.0)
    next_value = jnp.concatenate([value_est[1:], jnp.zeros((1,), jnp.float32)])
    not_last = 1.0 - is_last_flat.astype(jnp.float32)
    td_error = (reward + discount * next_value * not_last - value_est).reshape(shards, pair_len)
    decay = discount * gae_mix
    carry = td_error[:, pair_len - 1]
    columns = [carry]
    for step in range(pair_len - 2, -1, -1):
        carry = td_error[:, step] + decay * jnp.where(is_last[:, step], 0.0, carry)
        columns.append(carry)
    advantage = jnp.stack(columns[::-1], axis=1).reshape(-1)
    return (ref_logprob, advantage)


def solution(mesh):
    dp_devices = mesh.devices[:, 0]
    zs = sorted({d.coords[2] for d in dp_devices})
    xs = sorted({d.coords[0] for d in dp_devices})
    places = np.zeros((len(zs), len(xs)), np.int32)
    for i, d in enumerate(dp_devices):
        places[zs.index(d.coords[2]), xs.index(d.coords[0])] = i
    return jax.shard_map(
        functools.partial(body, places, source_tables(places)),
        mesh=mesh,
        in_specs=(
            P(),
            P(),
            P(),
            P("dp", None, "mp"),
            P("dp", None, "mp"),
            P("mp", "dp"),
            P("mp"),
            P("mp"),
            P("mp"),
            P("dp"),
        ),
        out_specs=(P("dp"), P("dp")),
        check_vma=False,
    )
```

```python
import jax
import jax.numpy as jnp
from jax import lax
from jax.experimental import pallas as pl
from jax.experimental.pallas import tpu as pltpu
from jax.sharding import PartitionSpec as P

kl_coef = 0.1
discount = 0.99
gae_mix = 0.95
norm_eps = 1e-05


def pair_rank(dest):
    count = dest.shape[-1]
    idx = jnp.arange(count, dtype=jnp.int32)
    same = dest[..., None, :] == dest[..., :, None]
    earlier = idx[None, :] < idx[:, None]
    return jnp.sum(jnp.logical_and(same, earlier).astype(jnp.int32), axis=-1)


def stats_kernel(heights, tile_n, target_ref, rows_ref, *refs):
    pieces = len(heights)
    weight_refs = refs[:pieces]
    max_ref, total_ref, target_logit_ref = refs[pieces:]
    logits = None
    offset = 0
    for k, height in enumerate(heights):
        part = jnp.dot(
            rows_ref[:, offset : offset + height], weight_refs[k][...], preferred_element_type=jnp.float32
        )
        logits = part if logits is None else logits + part
        offset += height
    row_max = jnp.max(logits, axis=1, keepdims=True)
    total = jnp.sum(jnp.exp(logits - row_max), axis=1, keepdims=True)
    column = lax.broadcasted_iota(jnp.int32, logits.shape, 1) + pl.program_id(0) * tile_n
    target_logit = jnp.sum(jnp.where(column == target_ref[...], logits, 0.0), axis=1, keepdims=True)
    max_ref[0] = row_max
    total_ref[0] = total
    target_logit_ref[0] = target_logit


def logit_stats(rows, pieces, local_target, tile_m=256, tile_n=1024):
    count, width_full = rows.shape
    vocab = pieces[0].shape[1]
    heights = tuple(piece.shape[0] for piece in pieces)
    grid = (vocab // tile_n, count // tile_m)
    stat_shape = jax.ShapeDtypeStruct((grid[0], count, 1), jnp.float32)
    stat_spec = pl.BlockSpec((1, tile_m, 1), lambda j, i: (j, i, 0))
    return pl.pallas_call(
        lambda *refs: stats_kernel(heights, tile_n, *refs),
        grid=grid,
        in_specs=[
            pl.BlockSpec((tile_m, 1), lambda j, i: (i, 0)),
            pl.BlockSpec((tile_m, width_full), lambda j, i: (i, 0)),
        ]
        + [pl.BlockSpec((height, tile_n), lambda j, i: (0, j)) for height in heights],
        out_specs=[stat_spec, stat_spec, stat_spec],
        out_shape=[stat_shape, stat_shape, stat_shape],
        compiler_params=pltpu.CompilerParams(vmem_limit_bytes=48 * 1024 * 1024),
        cost_estimate=pl.CostEstimate(
            flops=2 * count * width_full * vocab,
            transcendentals=count * vocab,
            bytes_accessed=2 * width_full * vocab + 2 * count * width_full * grid[0],
        ),
    )(local_target.reshape(count, 1), rows, *pieces)


def body(
    token_ids,
    lengths,
    pack_dest,
    ref_hidden,
    reward_hidden,
    head_weight,
    norm_gain,
    score_weight,
    value_weight,
    old_logprob,
):
    shards = lax.axis_size("dp")
    ways = lax.axis_size("mp")
    me = lax.axis_index("dp")
    part = lax.axis_index("mp")
    req_dev, max_len, width_dev = ref_hidden.shape
    pair_len = max_len + 1
    slot_dev = shards * pair_len
    sub_len = slot_dev // ways
    blocks = sub_len // pair_len
    width_full = width_dev * ways
    steps = jnp.arange(max_len, dtype=jnp.int32)

    dest = lax.dynamic_slice_in_dim(pack_dest, me * req_dev, req_dev)
    size = lax.dynamic_slice_in_dim(lengths, me * req_dev, req_dev)
    rank = pair_rank(dest)
    row = dest[:, None] * pair_len + steps[None, :] + rank[:, None] * (pair_len - size[:, None])
    row = jnp.where(steps[None, :] < size[:, None], row, -1).reshape(-1)
    onehot = (row[None, :] == jnp.arange(slot_dev, dtype=jnp.int32)[:, None]).astype(jnp.bfloat16)
    ref_send = jnp.dot(
        onehot, ref_hidden.reshape(req_dev * max_len, width_dev), preferred_element_type=jnp.float32
    ).astype(jnp.bfloat16)
    reward_send = jnp.dot(
        onehot, reward_hidden.reshape(req_dev * max_len, width_dev), preferred_element_type=jnp.float32
    ).astype(jnp.bfloat16)
    reward_packed = lax.all_to_all(
        reward_send.reshape(shards, pair_len, width_dev), "dp", 0, 0, tiled=True
    ).reshape(slot_dev, width_dev)

    chips = ways // 2
    half = width_dev // 2

    def along_y(x, shift):
        return lax.ppermute(x, "mp", [(i, ((i // 2 + shift) % chips) * 2 + i % 2) for i in range(ways)])

    from_prev = along_y(head_weight, 1)
    from_next = along_y(head_weight, -1)
    own_core = [
        head_weight,
        from_prev,
        from_next,
        along_y(from_prev[:half], 1),
        along_y(from_next[half:], -1),
    ]
    mate_core = [lax.ppermute(block, "mp", [(i, i ^ 1) for i in range(ways)]) for block in own_core]
    chip, core = part // 2, part % 2
    order = jnp.arange(ways, dtype=jnp.int32)
    chip_step = jnp.array([0, -1, 1, -2], jnp.int32)
    source_chip = (chip + chip_step[order % chips]) % chips
    source_core = jnp.where(order < chips, core, 1 - core)
    pick = (
        (source_chip * 2 + source_core)[:, None] == jnp.arange(ways, dtype=jnp.int32)[None, :]
    ).astype(jnp.bfloat16)

    parts_rows = lax.all_to_all(ref_send.reshape(ways, sub_len, width_dev), "mp", 0, 0, tiled=True)
    own_rows = jnp.einsum(
        "msf,nm->snf", parts_rows, pick, preferred_element_type=jnp.float32
    ).astype(jnp.bfloat16).reshape(sub_len, width_full)
    block_rows = lax.all_gather(own_rows, "dp", axis=0, tiled=True)

    dest_all = pack_dest.reshape(shards, req_dev)
    size_all = lengths.reshape(shards, req_dev)
    rank_all = pair_rank(dest_all)
    key = (
        dest_all[:, :, None] * pair_len
        + steps[None, None, :]
        + rank_all[:, :, None] * (pair_len - size_all[:, :, None])
        - part * sub_len
    )
    key = jnp.where(steps[None, None, :] < size_all[:, :, None], key, -1).reshape(shards, 1, -1)
    hits = key == jnp.arange(sub_len, dtype=jnp.int32)[None, :, None]
    targets = jnp.sum(
        jnp.where(hits, token_ids.reshape(shards, 1, -1), 0), axis=2
    ).reshape(-1)

    vocab_dev = head_weight.shape[1]
    tile_max, tile_total, tile_target = logit_stats(
        block_rows, own_core + mate_core, targets - me * vocab_dev
    )
    row_max = jnp.max(tile_max[:, :, 0], axis=0)
    exp_total = jnp.sum(tile_total[:, :, 0] * jnp.exp(tile_max[:, :, 0] - row_max[None, :]), axis=0)
    target_logit = jnp.sum(tile_target[:, :, 0], axis=0)
    stats = jnp.stack([row_max, exp_total, target_logit]).reshape(3, shards, blocks, pair_len)
    to_shard = jnp.arange(shards, dtype=jnp.int32)[:, None] == (
        part * blocks + jnp.arange(blocks, dtype=jnp.int32)
    )[None, :]
    routed = jnp.sum(
        jnp.where(to_shard[:, None, None, :, None], stats[None], 0.0), axis=3
    )
    routed = lax.all_to_all(routed, "dp", 0, 0, tiled=True)
    joint_max = jnp.max(routed[:, 0], axis=0)
    joint_total = jnp.sum(routed[:, 1] * jnp.exp(routed[:, 0] - joint_max[None]), axis=0)
    joint_target = jnp.sum(routed[:, 2], axis=0)
    holder = me // blocks == part
    block_logprob = jnp.where(
        holder, joint_target - joint_max - jnp.log(joint_total), 0.0
    ).reshape(-1)

    hidden_f = reward_packed.astype(jnp.float32)
    sums = jnp.stack(
        [
            jnp.sum(hidden_f * hidden_f, axis=1),
            jnp.sum(hidden_f * (norm_gain * score_weight), axis=1),
            jnp.sum(hidden_f * (norm_gain * value_weight), axis=1),
        ]
    )
    ref_logprob, squares, score_dot, value_dot = lax.psum(
        jnp.concatenate([block_logprob[None], sums]), "mp"
    )
    inv_rms = lax.rsqrt(squares / width_full + norm_eps)
    score = score_dot * inv_rms
    value_est = value_dot * inv_rms

    mine = (pack_dest.reshape(shards, req_dev) == me).astype(jnp.int32)
    is_first = jnp.logical_and(mine == 1, jnp.cumsum(mine, axis=1) == 1)
    first_len = jnp.sum(jnp.where(is_first, lengths.reshape(shards, req_dev), 0), axis=1)
    place = jnp.arange(pair_len, dtype=jnp.int32)[None, :]
    is_last = jnp.logical_or(place == first_len[:, None] - 1, place == pair_len - 1)
    is_last_flat = is_last.reshape(-1)

    reward = -kl_coef * (old_logprob - ref_logprob) + jnp.where(is_last_flat, score, 0.0)
    next_value = jnp.concatenate([value_est[1:], jnp.zeros((1,), jnp.float32)])
    not_last = 1.0 - is_last_flat.astype(jnp.float32)
    td_error = (reward + discount * next_value * not_last - value_est).reshape(shards, pair_len)
    decay = discount * gae_mix
    carry = td_error[:, pair_len - 1]
    columns = [carry]
    for step in range(pair_len - 2, -1, -1):
        carry = td_error[:, step] + decay * jnp.where(is_last[:, step], 0.0, carry)
        columns.append(carry)
    advantage = jnp.stack(columns[::-1], axis=1).reshape(-1)
    return (ref_logprob, advantage)


def solution(mesh):
    return jax.shard_map(
        body,
        mesh=mesh,
        in_specs=(
            P(),
            P(),
            P(),
            P("dp", None, "mp"),
            P("dp", None, "mp"),
            P("mp", "dp"),
            P("mp"),
            P("mp"),
            P("mp"),
            P("dp"),
        ),
        out_specs=(P("dp"), P("dp")),
        check_vma=False,
    )
```

```python
import jax
import jax.numpy as jnp
from jax import lax
from jax.experimental import pallas as pl
from jax.experimental.pallas import tpu as pltpu
from jax.sharding import PartitionSpec as P

kl_coef = 0.1
discount = 0.99
gae_mix = 0.95
norm_eps = 1e-05


def pair_rank(dest):
    count = dest.shape[-1]
    idx = jnp.arange(count, dtype=jnp.int32)
    same = dest[..., None, :] == dest[..., :, None]
    earlier = idx[None, :] < idx[:, None]
    return jnp.sum(jnp.logical_and(same, earlier).astype(jnp.int32), axis=-1)


def stats_kernel(heights, tile_n, target_ref, rows_ref, *refs):
    pieces = len(heights)
    weight_refs = refs[:pieces]
    max_ref, total_ref, target_logit_ref = refs[pieces:]
    logits = None
    offset = 0
    for k, height in enumerate(heights):
        part = jnp.dot(
            rows_ref[:, offset : offset + height], weight_refs[k][...], preferred_element_type=jnp.float32
        )
        logits = part if logits is None else logits + part
        offset += height
    row_max = jnp.max(logits, axis=1, keepdims=True)
    total = jnp.sum(jnp.exp(logits - row_max), axis=1, keepdims=True)
    column = lax.broadcasted_iota(jnp.int32, logits.shape, 1) + pl.program_id(0) * tile_n
    target_logit = jnp.sum(jnp.where(column == target_ref[...], logits, 0.0), axis=1, keepdims=True)
    max_ref[0] = row_max
    total_ref[0] = total
    target_logit_ref[0] = target_logit


def logit_stats(rows, pieces, local_target, tile_m=512, tile_n=1024):
    count, width_full = rows.shape
    vocab = pieces[0].shape[1]
    heights = tuple(piece.shape[0] for piece in pieces)
    grid = (vocab // tile_n, count // tile_m)
    stat_shape = jax.ShapeDtypeStruct((grid[0], count, 1), jnp.float32)
    stat_spec = pl.BlockSpec((1, tile_m, 1), lambda j, i: (j, i, 0))
    return pl.pallas_call(
        lambda *refs: stats_kernel(heights, tile_n, *refs),
        grid=grid,
        in_specs=[
            pl.BlockSpec((tile_m, 1), lambda j, i: (i, 0)),
            pl.BlockSpec((tile_m, width_full), lambda j, i: (i, 0)),
        ]
        + [pl.BlockSpec((height, tile_n), lambda j, i: (0, j)) for height in heights],
        out_specs=[stat_spec, stat_spec, stat_spec],
        out_shape=[stat_shape, stat_shape, stat_shape],
        compiler_params=pltpu.CompilerParams(vmem_limit_bytes=48 * 1024 * 1024),
        cost_estimate=pl.CostEstimate(
            flops=2 * count * width_full * vocab,
            transcendentals=count * vocab,
            bytes_accessed=2 * width_full * vocab + 2 * count * width_full * grid[0],
        ),
    )(local_target.reshape(count, 1), rows, *pieces)


def body(
    token_ids,
    lengths,
    pack_dest,
    ref_hidden,
    reward_hidden,
    head_weight,
    norm_gain,
    score_weight,
    value_weight,
    old_logprob,
):
    shards = lax.axis_size("dp")
    ways = lax.axis_size("mp")
    me = lax.axis_index("dp")
    part = lax.axis_index("mp")
    req_dev, max_len, width_dev = ref_hidden.shape
    pair_len = max_len + 1
    slot_dev = shards * pair_len
    sub_len = slot_dev // ways
    blocks = sub_len // pair_len
    width_full = width_dev * ways
    steps = jnp.arange(max_len, dtype=jnp.int32)

    dest = lax.dynamic_slice_in_dim(pack_dest, me * req_dev, req_dev)
    size = lax.dynamic_slice_in_dim(lengths, me * req_dev, req_dev)
    rank = pair_rank(dest)
    row = dest[:, None] * pair_len + steps[None, :] + rank[:, None] * (pair_len - size[:, None])
    row = jnp.where(steps[None, :] < size[:, None], row, -1).reshape(-1)
    onehot = (row[None, :] == jnp.arange(slot_dev, dtype=jnp.int32)[:, None]).astype(jnp.bfloat16)
    ref_send = jnp.dot(
        onehot, ref_hidden.reshape(req_dev * max_len, width_dev), preferred_element_type=jnp.float32
    ).astype(jnp.bfloat16)
    reward_send = jnp.dot(
        onehot, reward_hidden.reshape(req_dev * max_len, width_dev), preferred_element_type=jnp.float32
    ).astype(jnp.bfloat16)
    reward_packed = lax.all_to_all(
        reward_send.reshape(shards, pair_len, width_dev), "dp", 0, 0, tiled=True
    ).reshape(slot_dev, width_dev)

    chips = ways // 2
    half = width_dev // 2

    def along_y(x, shift):
        return lax.ppermute(x, "mp", [(i, ((i // 2 + shift) % chips) * 2 + i % 2) for i in range(ways)])

    from_prev = along_y(head_weight, 1)
    from_next = along_y(head_weight, -1)
    own_core = [
        head_weight,
        from_prev,
        from_next,
        along_y(from_prev[:half], 1),
        along_y(from_next[half:], -1),
    ]
    mate_core = [lax.ppermute(block, "mp", [(i, i ^ 1) for i in range(ways)]) for block in own_core]
    chip, core = part // 2, part % 2
    order = jnp.arange(ways, dtype=jnp.int32)
    chip_step = jnp.array([0, -1, 1, -2], jnp.int32)
    source_chip = (chip + chip_step[order % chips]) % chips
    source_core = jnp.where(order < chips, core, 1 - core)
    pick = (
        (source_chip * 2 + source_core)[:, None] == jnp.arange(ways, dtype=jnp.int32)[None, :]
    ).astype(jnp.bfloat16)

    parts_rows = lax.all_to_all(ref_send.reshape(ways, sub_len, width_dev), "mp", 0, 0, tiled=True)
    own_rows = jnp.einsum(
        "msf,nm->snf", parts_rows, pick, preferred_element_type=jnp.float32
    ).astype(jnp.bfloat16).reshape(sub_len, width_full)
    block_rows = lax.all_gather(own_rows, "dp", axis=0, tiled=True)

    dest_all = pack_dest.reshape(shards, req_dev)
    size_all = lengths.reshape(shards, req_dev)
    rank_all = pair_rank(dest_all)
    key = (
        dest_all[:, :, None] * pair_len
        + steps[None, None, :]
        + rank_all[:, :, None] * (pair_len - size_all[:, :, None])
        - part * sub_len
    )
    key = jnp.where(steps[None, None, :] < size_all[:, :, None], key, -1).reshape(shards, 1, -1)
    hits = key == jnp.arange(sub_len, dtype=jnp.int32)[None, :, None]
    targets = jnp.sum(
        jnp.where(hits, token_ids.reshape(shards, 1, -1), 0), axis=2
    ).reshape(-1)

    vocab_dev = head_weight.shape[1]
    tile_max, tile_total, tile_target = logit_stats(
        block_rows, own_core + mate_core, targets - me * vocab_dev
    )
    row_max = jnp.max(tile_max[:, :, 0], axis=0)
    exp_total = jnp.sum(tile_total[:, :, 0] * jnp.exp(tile_max[:, :, 0] - row_max[None, :]), axis=0)
    target_logit = jnp.sum(tile_target[:, :, 0], axis=0)
    stats = jnp.stack([row_max, exp_total, target_logit]).reshape(3, shards, blocks, pair_len)
    to_shard = jnp.arange(shards, dtype=jnp.int32)[:, None] == (
        part * blocks + jnp.arange(blocks, dtype=jnp.int32)
    )[None, :]
    routed = jnp.sum(
        jnp.where(to_shard[:, None, None, :, None], stats[None], 0.0), axis=3
    )
    routed = lax.all_to_all(routed, "dp", 0, 0, tiled=True)
    joint_max = jnp.max(routed[:, 0], axis=0)
    joint_total = jnp.sum(routed[:, 1] * jnp.exp(routed[:, 0] - joint_max[None]), axis=0)
    joint_target = jnp.sum(routed[:, 2], axis=0)
    holder = me // blocks == part
    block_logprob = jnp.where(
        holder, joint_target - joint_max - jnp.log(joint_total), 0.0
    ).reshape(-1)

    hidden_f = reward_packed.astype(jnp.float32)
    sums = jnp.stack(
        [
            jnp.sum(hidden_f * hidden_f, axis=1),
            jnp.sum(hidden_f * (norm_gain * score_weight), axis=1),
            jnp.sum(hidden_f * (norm_gain * value_weight), axis=1),
        ]
    )
    ref_logprob, squares, score_dot, value_dot = lax.psum(
        jnp.concatenate([block_logprob[None], sums]), "mp"
    )
    inv_rms = lax.rsqrt(squares / width_full + norm_eps)
    score = score_dot * inv_rms
    value_est = value_dot * inv_rms

    mine = (pack_dest.reshape(shards, req_dev) == me).astype(jnp.int32)
    is_first = jnp.logical_and(mine == 1, jnp.cumsum(mine, axis=1) == 1)
    first_len = jnp.sum(jnp.where(is_first, lengths.reshape(shards, req_dev), 0), axis=1)
    place = jnp.arange(pair_len, dtype=jnp.int32)[None, :]
    is_last = jnp.logical_or(place == first_len[:, None] - 1, place == pair_len - 1)
    is_last_flat = is_last.reshape(-1)

    reward = -kl_coef * (old_logprob - ref_logprob) + jnp.where(is_last_flat, score, 0.0)
    next_value = jnp.concatenate([value_est[1:], jnp.zeros((1,), jnp.float32)])
    not_last = 1.0 - is_last_flat.astype(jnp.float32)
    td_error = (reward + discount * next_value * not_last - value_est).reshape(shards, pair_len)
    decay = discount * gae_mix
    carry = td_error[:, pair_len - 1]
    columns = [carry]
    for step in range(pair_len - 2, -1, -1):
        carry = td_error[:, step] + decay * jnp.where(is_last[:, step], 0.0, carry)
        columns.append(carry)
    advantage = jnp.stack(columns[::-1], axis=1).reshape(-1)
    return (ref_logprob, advantage)


def solution(mesh):
    return jax.shard_map(
        body,
        mesh=mesh,
        in_specs=(
            P(),
            P(),
            P(),
            P("dp", None, "mp"),
            P("dp", None, "mp"),
            P("mp", "dp"),
            P("mp"),
            P("mp"),
            P("mp"),
            P("dp"),
        ),
        out_specs=(P("dp"), P("dp")),
        check_vma=False,
    )
```

```python
import jax
import jax.numpy as jnp
from jax import lax
from jax.experimental import pallas as pl
from jax.experimental.pallas import tpu as pltpu
from jax.sharding import PartitionSpec as P

kl_coef = 0.1
discount = 0.99
gae_mix = 0.95
norm_eps = 1e-05


def pair_rank(dest):
    count = dest.shape[-1]
    idx = jnp.arange(count, dtype=jnp.int32)
    same = dest[..., None, :] == dest[..., :, None]
    earlier = idx[None, :] < idx[:, None]
    return jnp.sum(jnp.logical_and(same, earlier).astype(jnp.int32), axis=-1)


def stats_kernel(heights, tile_n, target_ref, rows_ref, *refs):
    pieces = len(heights)
    weight_refs = refs[:pieces]
    max_ref, total_ref, target_logit_ref = refs[pieces:]
    logits = None
    offset = 0
    for k, height in enumerate(heights):
        part = jnp.dot(
            rows_ref[:, offset : offset + height], weight_refs[k][...], preferred_element_type=jnp.float32
        )
        logits = part if logits is None else logits + part
        offset += height
    row_max = jnp.max(logits, axis=1, keepdims=True)
    total = jnp.sum(jnp.exp(logits - row_max), axis=1, keepdims=True)
    column = lax.broadcasted_iota(jnp.int32, logits.shape, 1) + pl.program_id(0) * tile_n
    target_logit = jnp.sum(jnp.where(column == target_ref[...], logits, 0.0), axis=1, keepdims=True)
    max_ref[0] = row_max
    total_ref[0] = total
    target_logit_ref[0] = target_logit


def logit_stats(rows, pieces, local_target, tile_m=512, tile_n=1024):
    count, width_full = rows.shape
    vocab = pieces[0].shape[1]
    heights = tuple(piece.shape[0] for piece in pieces)
    grid = (vocab // tile_n, count // tile_m)
    stat_shape = jax.ShapeDtypeStruct((grid[0], count, 1), jnp.float32)
    stat_spec = pl.BlockSpec((1, tile_m, 1), lambda j, i: (j, i, 0))
    return pl.pallas_call(
        lambda *refs: stats_kernel(heights, tile_n, *refs),
        grid=grid,
        in_specs=[
            pl.BlockSpec((tile_m, 1), lambda j, i: (i, 0)),
            pl.BlockSpec((tile_m, width_full), lambda j, i: (i, 0)),
        ]
        + [pl.BlockSpec((height, tile_n), lambda j, i: (0, j)) for height in heights],
        out_specs=[stat_spec, stat_spec, stat_spec],
        out_shape=[stat_shape, stat_shape, stat_shape],
        compiler_params=pltpu.CompilerParams(vmem_limit_bytes=48 * 1024 * 1024),
        cost_estimate=pl.CostEstimate(
            flops=2 * count * width_full * vocab,
            transcendentals=count * vocab,
            bytes_accessed=2 * width_full * vocab + 2 * count * width_full * grid[0],
        ),
    )(local_target.reshape(count, 1), rows, *pieces)


def body(
    token_ids,
    lengths,
    pack_dest,
    ref_hidden,
    reward_hidden,
    head_weight,
    norm_gain,
    score_weight,
    value_weight,
    old_logprob,
):
    shards = lax.axis_size("dp")
    ways = lax.axis_size("mp")
    me = lax.axis_index("dp")
    part = lax.axis_index("mp")
    req_dev, max_len, width_dev = ref_hidden.shape
    pair_len = max_len + 1
    slot_dev = shards * pair_len
    sub_len = slot_dev // ways
    blocks = sub_len // pair_len
    width_full = width_dev * ways
    steps = jnp.arange(max_len, dtype=jnp.int32)

    dest = lax.dynamic_slice_in_dim(pack_dest, me * req_dev, req_dev)
    size = lax.dynamic_slice_in_dim(lengths, me * req_dev, req_dev)
    rank = pair_rank(dest)
    row = dest[:, None] * pair_len + steps[None, :] + rank[:, None] * (pair_len - size[:, None])
    row = jnp.where(steps[None, :] < size[:, None], row, -1).reshape(-1)
    onehot = (row[None, :] == jnp.arange(slot_dev, dtype=jnp.int32)[:, None]).astype(jnp.bfloat16)
    ref_send = jnp.dot(
        onehot, ref_hidden.reshape(req_dev * max_len, width_dev), preferred_element_type=jnp.float32
    ).astype(jnp.bfloat16)
    reward_send = jnp.dot(
        onehot, reward_hidden.reshape(req_dev * max_len, width_dev), preferred_element_type=jnp.float32
    ).astype(jnp.bfloat16)
    hidden_f = reward_send.astype(jnp.float32)
    partial = jnp.stack(
        [
            jnp.sum(hidden_f * hidden_f, axis=1),
            jnp.sum(hidden_f * (norm_gain * score_weight), axis=1),
            jnp.sum(hidden_f * (norm_gain * value_weight), axis=1),
        ],
        axis=1,
    )
    sums = lax.all_to_all(partial.reshape(shards, pair_len, 3), "dp", 0, 0, tiled=True)
    sums = sums.reshape(slot_dev, 3).T

    chips = ways // 2
    half = width_dev // 2

    def along_y(x, shift):
        return lax.ppermute(x, "mp", [(i, ((i // 2 + shift) % chips) * 2 + i % 2) for i in range(ways)])

    from_prev = along_y(head_weight, 1)
    from_next = along_y(head_weight, -1)
    own_core = [
        head_weight,
        from_prev,
        from_next,
        along_y(from_prev[:half], 1),
        along_y(from_next[half:], -1),
    ]
    mate_core = [lax.ppermute(block, "mp", [(i, i ^ 1) for i in range(ways)]) for block in own_core]
    chip, core = part // 2, part % 2
    order = jnp.arange(ways, dtype=jnp.int32)
    chip_step = jnp.array([0, -1, 1, -2], jnp.int32)
    source_chip = (chip + chip_step[order % chips]) % chips
    source_core = jnp.where(order < chips, core, 1 - core)
    pick = (
        (source_chip * 2 + source_core)[:, None] == jnp.arange(ways, dtype=jnp.int32)[None, :]
    ).astype(jnp.bfloat16)

    parts_rows = lax.all_to_all(ref_send.reshape(ways, sub_len, width_dev), "mp", 0, 0, tiled=True)
    own_rows = jnp.einsum(
        "msf,nm->snf", parts_rows, pick, preferred_element_type=jnp.float32
    ).astype(jnp.bfloat16).reshape(sub_len, width_full)
    block_rows = lax.all_gather(own_rows, "dp", axis=0, tiled=True)

    dest_all = pack_dest.reshape(shards, req_dev)
    size_all = lengths.reshape(shards, req_dev)
    rank_all = pair_rank(dest_all)
    key = (
        dest_all[:, :, None] * pair_len
        + steps[None, None, :]
        + rank_all[:, :, None] * (pair_len - size_all[:, :, None])
        - part * sub_len
    )
    key = jnp.where(steps[None, None, :] < size_all[:, :, None], key, -1).reshape(shards, 1, -1)
    hits = key == jnp.arange(sub_len, dtype=jnp.int32)[None, :, None]
    targets = jnp.sum(
        jnp.where(hits, token_ids.reshape(shards, 1, -1), 0), axis=2
    ).reshape(-1)

    vocab_dev = head_weight.shape[1]
    tile_max, tile_total, tile_target = logit_stats(
        block_rows, own_core + mate_core, targets - me * vocab_dev
    )
    row_max = jnp.max(tile_max[:, :, 0], axis=0)
    exp_total = jnp.sum(tile_total[:, :, 0] * jnp.exp(tile_max[:, :, 0] - row_max[None, :]), axis=0)
    target_logit = jnp.sum(tile_target[:, :, 0], axis=0)
    stats = jnp.stack([row_max, exp_total, target_logit]).reshape(3, shards, blocks, pair_len)
    to_shard = jnp.arange(shards, dtype=jnp.int32)[:, None] == (
        part * blocks + jnp.arange(blocks, dtype=jnp.int32)
    )[None, :]
    routed = jnp.sum(
        jnp.where(to_shard[:, None, None, :, None], stats[None], 0.0), axis=3
    )
    routed = lax.all_to_all(routed, "dp", 0, 0, tiled=True)
    joint_max = jnp.max(routed[:, 0], axis=0)
    joint_total = jnp.sum(routed[:, 1] * jnp.exp(routed[:, 0] - joint_max[None]), axis=0)
    joint_target = jnp.sum(routed[:, 2], axis=0)
    holder = me // blocks == part
    block_logprob = jnp.where(
        holder, joint_target - joint_max - jnp.log(joint_total), 0.0
    ).reshape(-1)

    ref_logprob, squares, score_dot, value_dot = lax.psum(
        jnp.concatenate([block_logprob[None], sums]), "mp"
    )
    inv_rms = lax.rsqrt(squares / width_full + norm_eps)
    score = score_dot * inv_rms
    value_est = value_dot * inv_rms

    mine = (pack_dest.reshape(shards, req_dev) == me).astype(jnp.int32)
    is_first = jnp.logical_and(mine == 1, jnp.cumsum(mine, axis=1) == 1)
    first_len = jnp.sum(jnp.where(is_first, lengths.reshape(shards, req_dev), 0), axis=1)
    place = jnp.arange(pair_len, dtype=jnp.int32)[None, :]
    is_last = jnp.logical_or(place == first_len[:, None] - 1, place == pair_len - 1)
    is_last_flat = is_last.reshape(-1)

    reward = -kl_coef * (old_logprob - ref_logprob) + jnp.where(is_last_flat, score, 0.0)
    next_value = jnp.concatenate([value_est[1:], jnp.zeros((1,), jnp.float32)])
    not_last = 1.0 - is_last_flat.astype(jnp.float32)
    td_error = (reward + discount * next_value * not_last - value_est).reshape(shards, pair_len)
    decay = discount * gae_mix
    carry = td_error[:, pair_len - 1]
    columns = [carry]
    for step in range(pair_len - 2, -1, -1):
        carry = td_error[:, step] + decay * jnp.where(is_last[:, step], 0.0, carry)
        columns.append(carry)
    advantage = jnp.stack(columns[::-1], axis=1).reshape(-1)
    return (ref_logprob, advantage)


def solution(mesh):
    return jax.shard_map(
        body,
        mesh=mesh,
        in_specs=(
            P(),
            P(),
            P(),
            P("dp", None, "mp"),
            P("dp", None, "mp"),
            P("mp", "dp"),
            P("mp"),
            P("mp"),
            P("mp"),
            P("dp"),
        ),
        out_specs=(P("dp"), P("dp")),
        check_vma=False,
    )
```

```python
import jax
import jax.numpy as jnp
from jax import lax
from jax.experimental import pallas as pl
from jax.experimental.pallas import tpu as pltpu
from jax.sharding import PartitionSpec as P

kl_coef = 0.1
discount = 0.99
gae_mix = 0.95
norm_eps = 1e-05


def pair_rank(dest):
    count = dest.shape[-1]
    idx = jnp.arange(count, dtype=jnp.int32)
    same = dest[..., None, :] == dest[..., :, None]
    earlier = idx[None, :] < idx[:, None]
    return jnp.sum(jnp.logical_and(same, earlier).astype(jnp.int32), axis=-1)


def stats_kernel(heights, tile_n, target_ref, rows_ref, *refs):
    pieces = len(heights)
    weight_refs = refs[:pieces]
    max_ref, total_ref, target_logit_ref = refs[pieces:]
    logits = None
    offset = 0
    for k, height in enumerate(heights):
        part = jnp.dot(
            rows_ref[:, offset : offset + height], weight_refs[k][...], preferred_element_type=jnp.float32
        )
        logits = part if logits is None else logits + part
        offset += height
    row_max = jnp.max(logits, axis=1, keepdims=True)
    total = jnp.sum(jnp.exp(logits - row_max), axis=1, keepdims=True)
    column = lax.broadcasted_iota(jnp.int32, logits.shape, 1) + pl.program_id(0) * tile_n
    target_logit = jnp.sum(jnp.where(column == target_ref[...], logits, 0.0), axis=1, keepdims=True)
    max_ref[0] = row_max
    total_ref[0] = total
    target_logit_ref[0] = target_logit


def logit_stats(rows, pieces, local_target, tile_m=1024, tile_n=512):
    count, width_full = rows.shape
    vocab = pieces[0].shape[1]
    heights = tuple(piece.shape[0] for piece in pieces)
    grid = (vocab // tile_n, count // tile_m)
    stat_shape = jax.ShapeDtypeStruct((grid[0], count, 1), jnp.float32)
    stat_spec = pl.BlockSpec((1, tile_m, 1), lambda j, i: (j, i, 0))
    return pl.pallas_call(
        lambda *refs: stats_kernel(heights, tile_n, *refs),
        grid=grid,
        in_specs=[
            pl.BlockSpec((tile_m, 1), lambda j, i: (i, 0)),
            pl.BlockSpec((tile_m, width_full), lambda j, i: (i, 0)),
        ]
        + [pl.BlockSpec((height, tile_n), lambda j, i: (0, j)) for height in heights],
        out_specs=[stat_spec, stat_spec, stat_spec],
        out_shape=[stat_shape, stat_shape, stat_shape],
        compiler_params=pltpu.CompilerParams(vmem_limit_bytes=48 * 1024 * 1024),
        cost_estimate=pl.CostEstimate(
            flops=2 * count * width_full * vocab,
            transcendentals=count * vocab,
            bytes_accessed=2 * width_full * vocab + 2 * count * width_full * grid[0],
        ),
    )(local_target.reshape(count, 1), rows, *pieces)


def body(
    token_ids,
    lengths,
    pack_dest,
    ref_hidden,
    reward_hidden,
    head_weight,
    norm_gain,
    score_weight,
    value_weight,
    old_logprob,
):
    shards = lax.axis_size("dp")
    ways = lax.axis_size("mp")
    me = lax.axis_index("dp")
    part = lax.axis_index("mp")
    req_dev, max_len, width_dev = ref_hidden.shape
    pair_len = max_len + 1
    slot_dev = shards * pair_len
    sub_len = slot_dev // ways
    blocks = sub_len // pair_len
    width_full = width_dev * ways
    steps = jnp.arange(max_len, dtype=jnp.int32)

    dest = lax.dynamic_slice_in_dim(pack_dest, me * req_dev, req_dev)
    size = lax.dynamic_slice_in_dim(lengths, me * req_dev, req_dev)
    rank = pair_rank(dest)
    row = dest[:, None] * pair_len + steps[None, :] + rank[:, None] * (pair_len - size[:, None])
    row = jnp.where(steps[None, :] < size[:, None], row, -1).reshape(-1)
    onehot = (row[None, :] == jnp.arange(slot_dev, dtype=jnp.int32)[:, None]).astype(jnp.bfloat16)
    ref_send = jnp.dot(
        onehot, ref_hidden.reshape(req_dev * max_len, width_dev), preferred_element_type=jnp.float32
    ).astype(jnp.bfloat16)
    reward_send = jnp.dot(
        onehot, reward_hidden.reshape(req_dev * max_len, width_dev), preferred_element_type=jnp.float32
    ).astype(jnp.bfloat16)
    hidden_f = reward_send.astype(jnp.float32)
    partial = jnp.stack(
        [
            jnp.sum(hidden_f * hidden_f, axis=1),
            jnp.sum(hidden_f * (norm_gain * score_weight), axis=1),
            jnp.sum(hidden_f * (norm_gain * value_weight), axis=1),
        ],
        axis=1,
    )
    sums = lax.all_to_all(partial.reshape(shards, pair_len, 3), "dp", 0, 0, tiled=True)
    sums = sums.reshape(slot_dev, 3).T

    chips = ways // 2
    half = width_dev // 2

    def along_y(x, shift):
        return lax.ppermute(x, "mp", [(i, ((i // 2 + shift) % chips) * 2 + i % 2) for i in range(ways)])

    from_prev = along_y(head_weight, 1)
    from_next = along_y(head_weight, -1)
    own_core = [
        head_weight,
        from_prev,
        from_next,
        along_y(from_prev[:half], 1),
        along_y(from_next[half:], -1),
    ]
    mate_core = [lax.ppermute(block, "mp", [(i, i ^ 1) for i in range(ways)]) for block in own_core]
    chip, core = part // 2, part % 2
    order = jnp.arange(ways, dtype=jnp.int32)
    chip_step = jnp.array([0, -1, 1, -2], jnp.int32)
    source_chip = (chip + chip_step[order % chips]) % chips
    source_core = jnp.where(order < chips, core, 1 - core)
    pick = (
        (source_chip * 2 + source_core)[:, None] == jnp.arange(ways, dtype=jnp.int32)[None, :]
    ).astype(jnp.bfloat16)

    parts_rows = lax.all_to_all(ref_send.reshape(ways, sub_len, width_dev), "mp", 0, 0, tiled=True)
    own_rows = jnp.einsum(
        "msf,nm->snf", parts_rows, pick, preferred_element_type=jnp.float32
    ).astype(jnp.bfloat16).reshape(sub_len, width_full)
    block_rows = lax.all_gather(own_rows, "dp", axis=0, tiled=True)

    dest_all = pack_dest.reshape(shards, req_dev)
    size_all = lengths.reshape(shards, req_dev)
    rank_all = pair_rank(dest_all)
    key = (
        dest_all[:, :, None] * pair_len
        + steps[None, None, :]
        + rank_all[:, :, None] * (pair_len - size_all[:, :, None])
        - part * sub_len
    )
    key = jnp.where(steps[None, None, :] < size_all[:, :, None], key, -1).reshape(shards, 1, -1)
    hits = key == jnp.arange(sub_len, dtype=jnp.int32)[None, :, None]
    targets = jnp.sum(
        jnp.where(hits, token_ids.reshape(shards, 1, -1), 0), axis=2
    ).reshape(-1)

    vocab_dev = head_weight.shape[1]
    tile_max, tile_total, tile_target = logit_stats(
        block_rows, own_core + mate_core, targets - me * vocab_dev
    )
    row_max = jnp.max(tile_max[:, :, 0], axis=0)
    exp_total = jnp.sum(tile_total[:, :, 0] * jnp.exp(tile_max[:, :, 0] - row_max[None, :]), axis=0)
    target_logit = jnp.sum(tile_target[:, :, 0], axis=0)
    stats = jnp.stack([row_max, exp_total, target_logit]).reshape(3, shards, blocks, pair_len)
    to_shard = jnp.arange(shards, dtype=jnp.int32)[:, None] == (
        part * blocks + jnp.arange(blocks, dtype=jnp.int32)
    )[None, :]
    routed = jnp.sum(
        jnp.where(to_shard[:, None, None, :, None], stats[None], 0.0), axis=3
    )
    routed = lax.all_to_all(routed, "dp", 0, 0, tiled=True)
    joint_max = jnp.max(routed[:, 0], axis=0)
    joint_total = jnp.sum(routed[:, 1] * jnp.exp(routed[:, 0] - joint_max[None]), axis=0)
    joint_target = jnp.sum(routed[:, 2], axis=0)
    holder = me // blocks == part
    block_logprob = jnp.where(
        holder, joint_target - joint_max - jnp.log(joint_total), 0.0
    ).reshape(-1)

    ref_logprob, squares, score_dot, value_dot = lax.psum(
        jnp.concatenate([block_logprob[None], sums]), "mp"
    )
    inv_rms = lax.rsqrt(squares / width_full + norm_eps)
    score = score_dot * inv_rms
    value_est = value_dot * inv_rms

    mine = (pack_dest.reshape(shards, req_dev) == me).astype(jnp.int32)
    is_first = jnp.logical_and(mine == 1, jnp.cumsum(mine, axis=1) == 1)
    first_len = jnp.sum(jnp.where(is_first, lengths.reshape(shards, req_dev), 0), axis=1)
    place = jnp.arange(pair_len, dtype=jnp.int32)[None, :]
    is_last = jnp.logical_or(place == first_len[:, None] - 1, place == pair_len - 1)
    is_last_flat = is_last.reshape(-1)

    reward = -kl_coef * (old_logprob - ref_logprob) + jnp.where(is_last_flat, score, 0.0)
    next_value = jnp.concatenate([value_est[1:], jnp.zeros((1,), jnp.float32)])
    not_last = 1.0 - is_last_flat.astype(jnp.float32)
    td_error = (reward + discount * next_value * not_last - value_est).reshape(shards, pair_len)
    decay = discount * gae_mix
    carry = td_error[:, pair_len - 1]
    columns = [carry]
    for step in range(pair_len - 2, -1, -1):
        carry = td_error[:, step] + decay * jnp.where(is_last[:, step], 0.0, carry)
        columns.append(carry)
    advantage = jnp.stack(columns[::-1], axis=1).reshape(-1)
    return (ref_logprob, advantage)


def solution(mesh):
    return jax.shard_map(
        body,
        mesh=mesh,
        in_specs=(
            P(),
            P(),
            P(),
            P("dp", None, "mp"),
            P("dp", None, "mp"),
            P("mp", "dp"),
            P("mp"),
            P("mp"),
            P("mp"),
            P("dp"),
        ),
        out_specs=(P("dp"), P("dp")),
        check_vma=False,
    )
```
